512 devices in a mesh: aux: 16 (over z), pair: 32 (over y, x, core).
Axes of the slice: x: 4, y: 4, z: 16, core: 2. Of those that a mesh axis runs over, the one named last changes fastest.
Arguments:
- b_tensor: bfloat16 [2560, 262144], P('aux', 'pair'), may hold values from -0.0625 to 0.0625
- eps_occ: float32 [256], replicated, may hold values from -1 to -0.3
- eps_vir: float32 [1024], replicated, may hold values from 0.05 to 3
- trial: bfloat16 [32, 262144], P(None, 'pair'), may hold values from -6 to 6
Outputs:
- trial_next: float32 [32, 262144], P(None, 'pair')
- residual: bfloat16 [32, 262144], P(None, 'pair')
- subspace: float32 [32, 32], replicated
The draws below stay inside these ranges and needn't reach their ends.
All inputs are finite; a program needn't handle non-finite values.
Results may differ from the reference program's by a relative error of at most 0.028.
Values may be sent and summed in bfloat16 or wider, within the bound.
No kernel may reach another device: no remote copies, remote signals or barrier semaphores. Data moves between devices by JAX's collectives and lax.ppermute only.
A program may use at most 64 MiB of HBM per device.

```python
import jax
import jax.numpy as jnp
from jax import lax

NOCC = 256
NVIR = 1024
NAUX = 2560
K = 32
ITERS = 2
NPAIR = 262144
N_AUX = 16


def block_levels(key, extent, cuts, smallest, top_value):
    level = 1.0
    for position, blocks in cuts:
        steps = jax.random.uniform(jax.random.fold_in(jax.random.fold_in(key, 6), position), (blocks,), jnp.float32, smallest / len(cuts), top_value / len(cuts))
        level = level * jnp.repeat(jnp.exp(steps), extent[position] // blocks).reshape((-1,) + (1,) * (len(extent) - 1 - position))
    return level


def bell_draw(key, shape, scale, reach, split=(), held_as=jnp.bfloat16):
    array = jax.random.normal(key, shape, jnp.float32) * scale
    if len(split) > 0:
        array = block_levels(key, shape, split, -0.22, 0.18) * array
    return jnp.clip(array, min=-reach, max=reach).astype(held_as)


def setup_inputs(seed: int = 0) -> dict:
    splits = jax.random.split(jax.random.key(seed), 5)
    b_tensor = bell_draw(splits[0], (NAUX, NPAIR), (4 * NAUX) ** -0.5, 0.0625, ((0, 16), (1, 32)))
    eps_occ = jnp.clip(jax.random.uniform(splits[1], (NOCC,), jnp.float32, -1.0, -0.3), -1.0, -0.3)
    eps_vir = jnp.clip(jax.random.uniform(splits[2], (NVIR,), jnp.float32, 0.05, 3.0), 0.05, 3.0)
    trial = bell_draw(splits[3], (K, NPAIR), 1.0, 6.0, ((1, 32),))
    return dict(b_tensor=b_tensor, eps_occ=eps_occ, eps_vir=eps_vir, trial=trial)


HIGHEST_PRECISION = lax.Precision.HIGHEST

def correlation_of(first_rows, second_rows):
    return lax.dot_general(first_rows.astype(jnp.float32), second_rows.astype(jnp.float32), (((1,), (1,)), ((), ())), precision=HIGHEST_PRECISION, preferred_element_type=jnp.float32)

def orthonormal(trial_now, gram_now):
    lower_tri = jnp.linalg.cholesky(gram_now)
    inverse = lax.linalg.triangular_solve(lower_tri, jnp.eye(gram_now.shape[0], dtype=jnp.float32), left_side=True, lower=True)
    return jnp.dot(inverse.astype(jnp.float32), trial_now.astype(jnp.float32), precision=HIGHEST_PRECISION, preferred_element_type=jnp.float32)

def add_group(running, members):
    block_rows, block_proj = members
    partial_value = lax.dot_general(block_proj.astype(jnp.float32), block_rows.astype(jnp.float32), (((0,), (0,)), ((), ())), preferred_element_type=jnp.float32)
    return (running + lax.optimization_barrier(partial_value.astype(jnp.bfloat16)).astype(jnp.float32), None)

def reference(b_tensor, eps_occ, eps_vir, trial):
    diagonal = (eps_vir[None, :] - eps_occ[:, None]).reshape(NPAIR)
    diag_row = diagonal[None, :]
    groups = b_tensor.reshape(N_AUX, NAUX // N_AUX, NPAIR)
    trial_now = trial.astype(jnp.float32)
    for iteration in range(ITERS):
        gram_now = correlation_of(trial_now, trial_now) / NPAIR
        basis_now = orthonormal(trial_now, gram_now)
        basis_low = basis_now.astype(jnp.bfloat16)
        projected = lax.dot_general(b_tensor.astype(jnp.float32), basis_low.astype(jnp.float32), (((1,), (1,)), ((), ())), preferred_element_type=jnp.float32)
        projected_low = projected.astype(jnp.bfloat16).reshape(N_AUX, NAUX // N_AUX, K)
        coupling, unused = lax.scan(add_group, jnp.zeros((K, NPAIR), jnp.float32), (groups, projected_low))
        image_now = coupling + diag_row * basis_now
        subspace = correlation_of(image_now, basis_now) / NPAIR
        residual = image_now - jnp.dot(subspace.astype(jnp.float32), basis_now.astype(jnp.float32), precision=HIGHEST_PRECISION, preferred_element_type=jnp.float32)
        trial_now = basis_now - residual / diag_row
    return (trial_now, residual.astype(jnp.bfloat16), subspace)
```

```python
import jax
import jax.numpy as jnp
from jax import lax
from jax.sharding import PartitionSpec as P

ITERS = 2


HIGHEST_PRECISION = lax.Precision.HIGHEST


def correlation_of(first_rows, second_rows, precision=HIGHEST_PRECISION):
    return lax.dot_general(
        first_rows,
        second_rows,
        (((1,), (1,)), ((), ())),
        precision=precision,
        preferred_element_type=jnp.float32,
    )


def product(first_mat, second_mat):
    return jnp.dot(
        first_mat, second_mat, precision=HIGHEST_PRECISION, preferred_element_type=jnp.float32
    )


def pair_sum(matrices):
    return lax.all_gather(matrices, "pair").sum(0)


def aux_sum(terms):
    n_aux = lax.axis_size("aux")
    rows, cols = terms.shape
    pieces = terms.reshape(rows, n_aux, cols // n_aux)
    pieces = lax.all_to_all(pieces, "aux", 1, 1, tiled=True)
    mine = pieces.astype(jnp.float32).sum(1)
    return lax.all_gather(mine, "aux", axis=1, tiled=True)


def inverse_factor(gram_now):
    lower_tri = jnp.linalg.cholesky(gram_now)
    return lax.linalg.triangular_solve(
        lower_tri, jnp.eye(gram_now.shape[0], dtype=jnp.float32), left_side=True, lower=True
    )


def on_device(b_tensor, eps_occ, eps_vir, trial):
    block_cols = b_tensor.shape[1]
    npair_all = eps_occ.shape[0] * eps_vir.shape[0]
    k = trial.shape[0]
    everything = (eps_vir[None, :] - eps_occ[:, None]).reshape(npair_all)
    diagonal = lax.dynamic_slice_in_dim(everything, lax.axis_index("pair") * block_cols, block_cols)
    diag_row = diagonal[None, :]
    trial_now = trial
    for iteration in range(ITERS):
        if iteration == 0:
            gram_part = correlation_of(trial_now, trial_now, None)
            cross_part = correlation_of(b_tensor, trial_now, None)
        else:
            gram_part = correlation_of(trial_now, trial_now)
            cross_part = correlation_of(b_tensor.astype(jnp.float32), trial_now)
        summed = pair_sum(jnp.concatenate([gram_part / npair_all, cross_part], axis=0))
        inverse = inverse_factor(summed[:k])
        basis_now = product(inverse, trial_now.astype(jnp.float32))
        projected = lax.dot_general(
            summed[k:], inverse, (((1,), (1,)), ((), ())),
            precision=HIGHEST_PRECISION, preferred_element_type=jnp.float32,
        )
        projected_low = projected.astype(jnp.bfloat16)
        term = lax.dot_general(
            projected_low, b_tensor, (((0,), (0,)), ((), ())), preferred_element_type=jnp.float32
        ).astype(jnp.bfloat16)
        image_now = aux_sum(term) + diag_row * basis_now
        subspace = pair_sum(correlation_of(image_now, basis_now) / npair_all)
        residual = image_now - product(subspace, basis_now)
        trial_now = basis_now - residual / diag_row
    return (trial_now, residual.astype(jnp.bfloat16), subspace)


def solution(mesh):
    in_specs = (P("aux", "pair"), P(), P(), P(None, "pair"))
    out_specs = (P(None, "pair"), P(None, "pair"), P())
    return jax.shard_map(
        on_device, mesh=mesh, in_specs=in_specs, out_specs=out_specs, check_vma=False
    )
```

```python
import jax
import jax.numpy as jnp
from jax import lax
from jax.sharding import PartitionSpec as P

ITERS = 2


HIGHEST_PRECISION = lax.Precision.HIGHEST


def correlation_of(first_rows, second_rows, precision=HIGHEST_PRECISION):
    return lax.dot_general(
        first_rows,
        second_rows,
        (((1,), (1,)), ((), ())),
        precision=precision,
        preferred_element_type=jnp.float32,
    )


def product(first_mat, second_mat):
    return jnp.dot(
        first_mat, second_mat, precision=HIGHEST_PRECISION, preferred_element_type=jnp.float32
    )


def pair_sum(matrices):
    return lax.all_gather(matrices, "pair").sum(0)


def aux_sum(terms):
    n_aux = lax.axis_size("aux")
    rows, cols = terms.shape
    pieces = terms.reshape(rows, n_aux, cols // n_aux)
    pieces = lax.all_to_all(pieces, "aux", 1, 1, tiled=True)
    mine = pieces.astype(jnp.float32).sum(1).astype(jnp.bfloat16)
    return lax.all_gather(mine, "aux", axis=1, tiled=True).astype(jnp.float32)


def inverse_factor(gram_now):
    lower_tri = jnp.linalg.cholesky(gram_now)
    return lax.linalg.triangular_solve(
        lower_tri, jnp.eye(gram_now.shape[0], dtype=jnp.float32), left_side=True, lower=True
    )


def on_device(b_tensor, eps_occ, eps_vir, trial):
    block_cols = b_tensor.shape[1]
    npair_all = eps_occ.shape[0] * eps_vir.shape[0]
    k = trial.shape[0]
    everything = (eps_vir[None, :] - eps_occ[:, None]).reshape(npair_all)
    diagonal = lax.dynamic_slice_in_dim(everything, lax.axis_index("pair") * block_cols, block_cols)
    diag_row = diagonal[None, :]
    trial_now = trial
    for iteration in range(ITERS):
        precision = None if iteration == 0 else HIGHEST_PRECISION
        wide_trial = trial_now.astype(jnp.float32)
        gram_part = correlation_of(trial_now, trial_now, precision)
        weighted_part = correlation_of(wide_trial * diag_row, wide_trial)
        cross_part = correlation_of(b_tensor.astype(wide_trial.dtype) if precision else b_tensor,
                                    trial_now, precision)
        summed = pair_sum(jnp.concatenate(
            [gram_part / npair_all, weighted_part / npair_all, cross_part], axis=0))
        inverse = inverse_factor(summed[:k])
        basis_now = product(inverse, wide_trial)
        projected = lax.dot_general(
            summed[2 * k:], inverse, (((1,), (1,)), ((), ())),
            precision=HIGHEST_PRECISION, preferred_element_type=jnp.float32,
        )
        group_part = lax.dot_general(
            projected, projected, (((0,), (0,)), ((), ())),
            precision=HIGHEST_PRECISION, preferred_element_type=jnp.float32,
        )
        group_sum = lax.all_gather(group_part / npair_all, "aux").sum(0)
        diag_part = product(product(inverse, summed[k:2 * k]), inverse.T)
        subspace = group_sum + diag_part
        projected_low = projected.astype(jnp.bfloat16)
        term = lax.dot_general(
            projected_low, b_tensor, (((0,), (0,)), ((), ())), preferred_element_type=jnp.float32
        ).astype(jnp.bfloat16)
        image_now = aux_sum(term) + diag_row * basis_now
        residual = image_now - product(subspace, basis_now)
        trial_now = basis_now - residual / diag_row
    return (trial_now, residual.astype(jnp.bfloat16), subspace)


def solution(mesh):
    in_specs = (P("aux", "pair"), P(), P(), P(None, "pair"))
    out_specs = (P(None, "pair"), P(None, "pair"), P())
    return jax.shard_map(
        on_device, mesh=mesh, in_specs=in_specs, out_specs=out_specs, check_vma=False
    )
```

```python
import jax
import jax.numpy as jnp
from jax import lax
from jax.sharding import PartitionSpec as P

ITERS = 2


HIGHEST_PRECISION = lax.Precision.HIGHEST


def correlation_of(first_rows, second_rows, precision=HIGHEST_PRECISION):
    return lax.dot_general(
        first_rows,
        second_rows,
        (((1,), (1,)), ((), ())),
        precision=precision,
        preferred_element_type=jnp.float32,
    )


def product(first_mat, second_mat):
    return jnp.dot(
        first_mat, second_mat, precision=HIGHEST_PRECISION, preferred_element_type=jnp.float32
    )


def pair_sum(matrices):
    return lax.all_gather(matrices, "pair").sum(0)


def aux_sum(terms, small):
    n_aux = lax.axis_size("aux")
    rows, cols = terms.shape
    high = small.astype(jnp.bfloat16)
    low = (small - high.astype(jnp.float32)).astype(jnp.bfloat16)
    extra = jnp.concatenate([high, low], axis=1)
    pieces = jnp.concatenate([
        terms.reshape(rows, n_aux, cols // n_aux),
        jnp.broadcast_to(extra[:, None, :], (rows, n_aux, extra.shape[1])),
    ], axis=2)
    pieces = lax.all_to_all(pieces, "aux", 1, 1, tiled=True)
    mine = pieces[:, :, : cols // n_aux].astype(jnp.float32).sum(1).astype(jnp.bfloat16)
    parts = pieces[:, :, cols // n_aux:].astype(jnp.float32)
    width = small.shape[1]
    small_sum = (parts[:, :, :width] + parts[:, :, width:]).sum(1)
    return lax.all_gather(mine, "aux", axis=1, tiled=True).astype(jnp.float32), small_sum


def inverse_factor(gram_now):
    lower_tri = jnp.linalg.cholesky(gram_now)
    return lax.linalg.triangular_solve(
        lower_tri, jnp.eye(gram_now.shape[0], dtype=jnp.float32), left_side=True, lower=True
    )


def on_device(b_tensor, eps_occ, eps_vir, trial):
    block_cols = b_tensor.shape[1]
    npair_all = eps_occ.shape[0] * eps_vir.shape[0]
    k = trial.shape[0]
    everything = (eps_vir[None, :] - eps_occ[:, None]).reshape(npair_all)
    diagonal = lax.dynamic_slice_in_dim(everything, lax.axis_index("pair") * block_cols, block_cols)
    diag_row = diagonal[None, :]
    trial_now = trial
    for iteration in range(ITERS):
        precision = None if iteration == 0 else HIGHEST_PRECISION
        wide_trial = trial_now.astype(jnp.float32)
        gram_part = correlation_of(trial_now, trial_now, precision)
        weighted_part = correlation_of(wide_trial * diag_row, wide_trial)
        cross_part = correlation_of(b_tensor.astype(wide_trial.dtype) if precision else b_tensor,
                                    trial_now, precision)
        summed = pair_sum(jnp.concatenate(
            [gram_part / npair_all, weighted_part / npair_all, cross_part], axis=0))
        inverse = inverse_factor(summed[:k])
        basis_now = product(inverse, wide_trial)
        projected = lax.dot_general(
            summed[2 * k:], inverse, (((1,), (1,)), ((), ())),
            precision=HIGHEST_PRECISION, preferred_element_type=jnp.float32,
        )
        group_part = lax.dot_general(
            projected, projected, (((0,), (0,)), ((), ())),
            precision=HIGHEST_PRECISION, preferred_element_type=jnp.float32,
        )
        diag_part = product(product(inverse, summed[k:2 * k]), inverse.T)
        projected_low = projected.astype(jnp.bfloat16)
        term = lax.dot_general(
            projected_low, b_tensor, (((0,), (0,)), ((), ())), preferred_element_type=jnp.float32
        ).astype(jnp.bfloat16)
        coupling, group_sum = aux_sum(term, group_part / npair_all)
        subspace = group_sum + diag_part
        image_now = coupling + diag_row * basis_now
        residual = image_now - product(subspace, basis_now)
        trial_now = basis_now - residual / diag_row
    return (trial_now, residual.astype(jnp.bfloat16), subspace)


def solution(mesh):
    in_specs = (P("aux", "pair"), P(), P(), P(None, "pair"))
    out_specs = (P(None, "pair"), P(None, "pair"), P())
    return jax.shard_map(
        on_device, mesh=mesh, in_specs=in_specs, out_specs=out_specs, check_vma=False
    )
```

```python
import jax
import jax.numpy as jnp
from jax import lax
from jax.sharding import PartitionSpec as P

ITERS = 2


HIGHEST_PRECISION = lax.Precision.HIGHEST


def correlation_of(first_rows, second_rows, precision=HIGHEST_PRECISION):
    return lax.dot_general(
        first_rows,
        second_rows,
        (((1,), (1,)), ((), ())),
        precision=precision,
        preferred_element_type=jnp.float32,
    )


def product(first_mat, second_mat):
    return jnp.dot(
        first_mat, second_mat, precision=HIGHEST_PRECISION, preferred_element_type=jnp.float32
    )


def pair_sum(matrices):
    return lax.all_gather(matrices, "pair").sum(0)


def aux_sum(terms, small):
    n_aux = lax.axis_size("aux")
    rows, cols = terms.shape
    high = small.astype(jnp.bfloat16)
    low = (small - high.astype(jnp.float32)).astype(jnp.bfloat16)
    extra = jnp.concatenate([high, low], axis=1)
    pieces = jnp.concatenate([
        terms.reshape(rows, n_aux, cols // n_aux),
        jnp.broadcast_to(extra[:, None, :], (rows, n_aux, extra.shape[1])),
    ], axis=2)
    pieces = lax.all_to_all(pieces, "aux", 1, 1, tiled=True)
    mine = pieces[:, :, : cols // n_aux].astype(jnp.float32).sum(1).astype(jnp.bfloat16)
    parts = pieces[:, :, cols // n_aux:].astype(jnp.float32)
    width = small.shape[1]
    small_sum = (parts[:, :, :width] + parts[:, :, width:]).sum(1)
    return lax.all_gather(mine, "aux", axis=1, tiled=True).astype(jnp.float32), small_sum


def inverse_factor(gram_now):
    lower_tri = jnp.linalg.cholesky(gram_now)
    return lax.linalg.triangular_solve(
        lower_tri, jnp.eye(gram_now.shape[0], dtype=jnp.float32), left_side=True, lower=True
    )


def on_device(b_tensor, eps_occ, eps_vir, trial):
    block_cols = b_tensor.shape[1]
    npair_all = eps_occ.shape[0] * eps_vir.shape[0]
    k = trial.shape[0]
    nvir = eps_vir.shape[0]
    if block_cols % nvir == 0:
        occ_rows = block_cols // nvir
        occ_block = lax.dynamic_slice_in_dim(eps_occ, lax.axis_index("pair") * occ_rows, occ_rows)
        diagonal = (eps_vir[None, :] - occ_block[:, None]).reshape(block_cols)
    else:
        everything = (eps_vir[None, :] - eps_occ[:, None]).reshape(npair_all)
        diagonal = lax.dynamic_slice_in_dim(
            everything, lax.axis_index("pair") * block_cols, block_cols)
    diag_row = diagonal[None, :]
    trial_now = trial
    for iteration in range(ITERS):
        precision = None if iteration == 0 else HIGHEST_PRECISION
        wide_trial = trial_now.astype(jnp.float32)
        gram_part = correlation_of(trial_now, trial_now, precision)
        weighted_part = correlation_of(wide_trial * diag_row, wide_trial)
        if precision is None:
            cross_part = correlation_of(b_tensor, trial_now, None)
        else:
            high = trial_now.astype(jnp.bfloat16)
            low = (trial_now - high.astype(jnp.float32)).astype(jnp.bfloat16)
            cross_part = (correlation_of(b_tensor, high, None)
                          + correlation_of(b_tensor, low, None))
        summed = pair_sum(jnp.concatenate(
            [gram_part / npair_all, weighted_part / npair_all, cross_part], axis=0))
        inverse = inverse_factor(summed[:k])
        basis_now = product(inverse, wide_trial)
        projected = lax.dot_general(
            summed[2 * k:], inverse, (((1,), (1,)), ((), ())),
            precision=HIGHEST_PRECISION, preferred_element_type=jnp.float32,
        )
        group_part = lax.dot_general(
            projected, projected, (((0,), (0,)), ((), ())),
            precision=HIGHEST_PRECISION, preferred_element_type=jnp.float32,
        )
        diag_part = product(product(inverse, summed[k:2 * k]), inverse.T)
        projected_low = projected.astype(jnp.bfloat16)
        term = lax.dot_general(
            projected_low, b_tensor, (((0,), (0,)), ((), ())), preferred_element_type=jnp.float32
        ).astype(jnp.bfloat16)
        coupling, group_sum = aux_sum(term, group_part / npair_all)
        subspace = group_sum + diag_part
        image_now = coupling + diag_row * basis_now
        residual = image_now - product(subspace, basis_now)
        trial_now = basis_now - residual / diag_row
    return (trial_now, residual.astype(jnp.bfloat16), subspace)


def solution(mesh):
    in_specs = (P("aux", "pair"), P(), P(), P(None, "pair"))
    out_specs = (P(None, "pair"), P(None, "pair"), P())
    return jax.shard_map(
        on_device, mesh=mesh, in_specs=in_specs, out_specs=out_specs, check_vma=False
    )
```

```python
import jax
import jax.numpy as jnp
from jax import lax
from jax.sharding import PartitionSpec as P
from jax.experimental import pallas as pl
from jax.experimental.pallas import tpu as pltpu

ITERS = 2


HIGHEST_PRECISION = lax.Precision.HIGHEST


def correlation_of(first_rows, second_rows, precision=HIGHEST_PRECISION):
    return lax.dot_general(
        first_rows,
        second_rows,
        (((1,), (1,)), ((), ())),
        precision=precision,
        preferred_element_type=jnp.float32,
    )


def product(first_mat, second_mat):
    return jnp.dot(
        first_mat, second_mat, precision=HIGHEST_PRECISION, preferred_element_type=jnp.float32
    )


def pair_sum(matrices):
    return lax.all_gather(matrices, "pair").sum(0)


def aux_sum(terms, small):
    n_aux = lax.axis_size("aux")
    rows, cols = terms.shape
    high = small.astype(jnp.bfloat16)
    low = (small - high.astype(jnp.float32)).astype(jnp.bfloat16)
    extra = jnp.concatenate([high, low], axis=1)
    pieces = jnp.concatenate([
        terms.reshape(rows, n_aux, cols // n_aux),
        jnp.broadcast_to(extra[:, None, :], (rows, n_aux, extra.shape[1])),
    ], axis=2)
    pieces = lax.all_to_all(pieces, "aux", 1, 1, tiled=True)
    mine = pieces[:, :, : cols // n_aux].astype(jnp.float32).sum(1).astype(jnp.bfloat16)
    parts = pieces[:, :, cols // n_aux:].astype(jnp.float32)
    width = small.shape[1]
    small_sum = (parts[:, :, :width] + parts[:, :, width:]).sum(1)
    return lax.all_gather(mine, "aux", axis=1, tiled=True).astype(jnp.float32), small_sum


def _inverse_factor_kernel(gram_ref, inverse_ref):
    work = gram_ref[...]
    k = work.shape[0]
    rows = lax.broadcasted_iota(jnp.int32, (k, k), 0)
    lanes = lax.broadcasted_iota(jnp.int32, (k, k), 1)
    row_ids = lax.broadcasted_iota(jnp.int32, (k, 1), 0)
    lane_ids = lax.broadcasted_iota(jnp.int32, (1, k), 1)
    inverse = (rows == lanes).astype(jnp.float32)
    for j in range(k):
        pick = rows == j
        column = jnp.sum(jnp.where(lanes == j, work, 0.0), axis=1, keepdims=True)
        work_row = jnp.sum(jnp.where(pick, work, 0.0), axis=0, keepdims=True)
        inverse_row = jnp.sum(jnp.where(pick, inverse, 0.0), axis=0, keepdims=True)
        pivot = jnp.sum(jnp.where(lane_ids == j, work_row, 0.0), axis=1, keepdims=True)
        scale = 1.0 / jnp.sqrt(pivot)
        work_row = work_row * scale
        inverse_row = inverse_row * scale
        factor = jnp.where(row_ids > j, column * scale, 0.0)
        work = jnp.where(pick, work_row, work - factor * work_row)
        inverse = jnp.where(pick, inverse_row, inverse - factor * inverse_row)
    inverse_ref[...] = inverse

def inverse_factor(gram_now):
    k = gram_now.shape[0]
    return pl.pallas_call(
        _inverse_factor_kernel,
        out_shape=jax.ShapeDtypeStruct((k, k), jnp.float32),
        in_specs=[pl.BlockSpec(memory_space=pltpu.VMEM)],
        out_specs=pl.BlockSpec(memory_space=pltpu.VMEM),
    )(gram_now)


def on_device(b_tensor, eps_occ, eps_vir, trial):
    block_cols = b_tensor.shape[1]
    npair_all = eps_occ.shape[0] * eps_vir.shape[0]
    k = trial.shape[0]
    nvir = eps_vir.shape[0]
    if block_cols % nvir == 0:
        occ_rows = block_cols // nvir
        occ_block = lax.dynamic_slice_in_dim(eps_occ, lax.axis_index("pair") * occ_rows, occ_rows)
        diagonal = (eps_vir[None, :] - occ_block[:, None]).reshape(block_cols)
    else:
        everything = (eps_vir[None, :] - eps_occ[:, None]).reshape(npair_all)
        diagonal = lax.dynamic_slice_in_dim(
            everything, lax.axis_index("pair") * block_cols, block_cols)
    diag_row = diagonal[None, :]
    trial_now = trial
    for iteration in range(ITERS):
        precision = None if iteration == 0 else HIGHEST_PRECISION
        wide_trial = trial_now.astype(jnp.float32)
        gram_part = correlation_of(trial_now, trial_now, precision)
        weighted_part = correlation_of(wide_trial * diag_row, wide_trial)
        if precision is None:
            cross_part = correlation_of(b_tensor, trial_now, None)
        else:
            high = trial_now.astype(jnp.bfloat16)
            low = (trial_now - high.astype(jnp.float32)).astype(jnp.bfloat16)
            cross_part = (correlation_of(b_tensor, high, None)
                          + correlation_of(b_tensor, low, None))
        summed = pair_sum(jnp.concatenate(
            [gram_part / npair_all, weighted_part / npair_all, cross_part], axis=0))
        inverse = inverse_factor(summed[:k])
        basis_now = product(inverse, wide_trial)
        projected = lax.dot_general(
            summed[2 * k:], inverse, (((1,), (1,)), ((), ())),
            precision=HIGHEST_PRECISION, preferred_element_type=jnp.float32,
        )
        group_part = lax.dot_general(
            projected, projected, (((0,), (0,)), ((), ())),
            precision=HIGHEST_PRECISION, preferred_element_type=jnp.float32,
        )
        diag_part = product(product(inverse, summed[k:2 * k]), inverse.T)
        projected_low = projected.astype(jnp.bfloat16)
        term = lax.dot_general(
            projected_low, b_tensor, (((0,), (0,)), ((), ())), preferred_element_type=jnp.float32
        ).astype(jnp.bfloat16)
        coupling, group_sum = aux_sum(term, group_part / npair_all)
        subspace = group_sum + diag_part
        image_now = coupling + diag_row * basis_now
        residual = image_now - product(subspace, basis_now)
        trial_now = basis_now - residual / diag_row
    return (trial_now, residual.astype(jnp.bfloat16), subspace)


def solution(mesh):
    in_specs = (P("aux", "pair"), P(), P(), P(None, "pair"))
    out_specs = (P(None, "pair"), P(None, "pair"), P())
    return jax.shard_map(
        on_device, mesh=mesh, in_specs=in_specs, out_specs=out_specs, check_vma=False
    )
```

```python
import jax
import jax.numpy as jnp
from jax import lax
from jax.sharding import PartitionSpec as P
from jax.experimental import pallas as pl
from jax.experimental.pallas import tpu as pltpu

ITERS = 2


HIGHEST_PRECISION = lax.Precision.HIGHEST


def correlation_of(first_rows, second_rows, precision=HIGHEST_PRECISION):
    return lax.dot_general(
        first_rows,
        second_rows,
        (((1,), (1,)), ((), ())),
        precision=precision,
        preferred_element_type=jnp.float32,
    )


def product(first_mat, second_mat):
    return jnp.dot(
        first_mat, second_mat, precision=HIGHEST_PRECISION, preferred_element_type=jnp.float32
    )


def pair_sum(matrices):
    return lax.all_gather(matrices, "pair").sum(0)


def aux_sum(terms, small):
    n_aux = lax.axis_size("aux")
    rows, cols = terms.shape
    high = small.astype(jnp.bfloat16)
    low = (small - high.astype(jnp.float32)).astype(jnp.bfloat16)
    extra = jnp.concatenate([high, low], axis=1)
    pieces = jnp.concatenate([
        terms.reshape(rows, n_aux, cols // n_aux),
        jnp.broadcast_to(extra[:, None, :], (rows, n_aux, extra.shape[1])),
    ], axis=2)
    pieces = lax.all_to_all(pieces, "aux", 1, 1, tiled=True)
    mine = pieces[:, :, : cols // n_aux].astype(jnp.float32).sum(1).astype(jnp.bfloat16)
    parts = pieces[:, :, cols // n_aux:].astype(jnp.float32)
    width = small.shape[1]
    small_sum = (parts[:, :, :width] + parts[:, :, width:]).sum(1)
    return lax.all_gather(mine, "aux", axis=1, tiled=True).astype(jnp.float32), small_sum


def _inverse_factor_kernel(gram_ref, inverse_ref):
    work = gram_ref[...]
    k = work.shape[0]
    rows = lax.broadcasted_iota(jnp.int32, (k, k), 0)
    lanes = lax.broadcasted_iota(jnp.int32, (k, k), 1)
    row_ids = lax.broadcasted_iota(jnp.int32, (k, 1), 0)
    lane_ids = lax.broadcasted_iota(jnp.int32, (1, k), 1)
    inverse = (rows == lanes).astype(jnp.float32)
    for j in range(k):
        pick = rows == j
        column = jnp.sum(jnp.where(lanes == j, work, 0.0), axis=1, keepdims=True)
        work_row = jnp.sum(jnp.where(pick, work, 0.0), axis=0, keepdims=True)
        inverse_row = jnp.sum(jnp.where(pick, inverse, 0.0), axis=0, keepdims=True)
        pivot = jnp.sum(jnp.where(lane_ids == j, work_row, 0.0), axis=1, keepdims=True)
        scale = 1.0 / jnp.sqrt(pivot)
        work_row = work_row * scale
        inverse_row = inverse_row * scale
        factor = jnp.where(row_ids > j, column * scale, 0.0)
        work = jnp.where(pick, work_row, work - factor * work_row)
        inverse = jnp.where(pick, inverse_row, inverse - factor * inverse_row)
    inverse_ref[...] = inverse

def inverse_factor(gram_now):
    k = gram_now.shape[0]
    return pl.pallas_call(
        _inverse_factor_kernel,
        out_shape=jax.ShapeDtypeStruct((k, k), jnp.float32),
        in_specs=[pl.BlockSpec(memory_space=pltpu.VMEM)],
        out_specs=pl.BlockSpec(memory_space=pltpu.VMEM),
    )(gram_now)


def on_device(b_tensor, eps_occ, eps_vir, trial):
    block_cols = b_tensor.shape[1]
    npair_all = eps_occ.shape[0] * eps_vir.shape[0]
    k = trial.shape[0]
    nvir = eps_vir.shape[0]
    if block_cols % nvir == 0:
        occ_rows = block_cols // nvir
        occ_block = lax.dynamic_slice_in_dim(eps_occ, lax.axis_index("pair") * occ_rows, occ_rows)
        diagonal = (eps_vir[None, :] - occ_block[:, None]).reshape(block_cols)
    else:
        everything = (eps_vir[None, :] - eps_occ[:, None]).reshape(npair_all)
        diagonal = lax.dynamic_slice_in_dim(
            everything, lax.axis_index("pair") * block_cols, block_cols)
    diag_row = diagonal[None, :]
    trial_now = trial
    for iteration in range(ITERS):
        wide_trial = trial_now.astype(jnp.float32)
        weighted = wide_trial * diag_row
        weighted_high = weighted.astype(jnp.bfloat16)
        weighted_low = (weighted - weighted_high.astype(jnp.float32)).astype(jnp.bfloat16)
        if iteration == 0:
            both = correlation_of(
                jnp.concatenate([trial_now, weighted_high, weighted_low], axis=0), trial_now, None)
            gram_part = both[:k]
            weighted_part = both[k:2 * k] + both[2 * k:]
            cross_part = correlation_of(b_tensor, trial_now, None)
        else:
            high = trial_now.astype(jnp.bfloat16)
            low = (trial_now - high.astype(jnp.float32)).astype(jnp.bfloat16)
            split = jnp.concatenate([high, low], axis=0)
            both = correlation_of(
                jnp.concatenate([high, low, weighted_high, weighted_low], axis=0), split, None)
            gram_part = both[:k, :k] + both[:k, k:] + both[k:2 * k, :k]
            weighted_part = both[2 * k:3 * k, :k] + both[2 * k:3 * k, k:] + both[3 * k:, :k]
            cross = correlation_of(b_tensor, split, None)
            cross_part = cross[:, :k] + cross[:, k:]
        summed = pair_sum(jnp.concatenate(
            [gram_part / npair_all, weighted_part / npair_all, cross_part], axis=0))
        inverse = inverse_factor(summed[:k])
        basis_now = product(inverse, wide_trial)
        projected = lax.dot_general(
            summed[2 * k:], inverse, (((1,), (1,)), ((), ())),
            precision=HIGHEST_PRECISION, preferred_element_type=jnp.float32,
        )
        group_part = lax.dot_general(
            projected, projected, (((0,), (0,)), ((), ())),
            precision=HIGHEST_PRECISION, preferred_element_type=jnp.float32,
        )
        diag_part = product(product(inverse, summed[k:2 * k]), inverse.T)
        projected_low = projected.astype(jnp.bfloat16)
        term = lax.dot_general(
            projected_low, b_tensor, (((0,), (0,)), ((), ())), preferred_element_type=jnp.float32
        ).astype(jnp.bfloat16)
        coupling, group_sum = aux_sum(term, group_part / npair_all)
        subspace = group_sum + diag_part
        image_now = coupling + diag_row * basis_now
        residual = image_now - product(subspace, basis_now)
        trial_now = basis_now - residual / diag_row
    return (trial_now, residual.astype(jnp.bfloat16), subspace)


def solution(mesh):
    in_specs = (P("aux", "pair"), P(), P(), P(None, "pair"))
    out_specs = (P(None, "pair"), P(None, "pair"), P())
    return jax.shard_map(
        on_device, mesh=mesh, in_specs=in_specs, out_specs=out_specs, check_vma=False
    )
```

```python
import jax
import jax.numpy as jnp
from jax import lax
from jax.sharding import PartitionSpec as P
from jax.experimental import pallas as pl
from jax.experimental.pallas import tpu as pltpu

ITERS = 2


HIGHEST_PRECISION = lax.Precision.HIGHEST


def correlation_of(first_rows, second_rows, precision=HIGHEST_PRECISION):
    return lax.dot_general(
        first_rows,
        second_rows,
        (((1,), (1,)), ((), ())),
        precision=precision,
        preferred_element_type=jnp.float32,
    )


def product(first_mat, second_mat):
    return jnp.dot(
        first_mat, second_mat, precision=HIGHEST_PRECISION, preferred_element_type=jnp.float32
    )


def pair_sum(matrices):
    return lax.all_gather(matrices, "pair").sum(0)


def aux_sum(terms):
    n_aux = lax.axis_size("aux")
    rows, cols = terms.shape
    pieces = terms.reshape(rows, n_aux, cols // n_aux)
    pieces = lax.all_to_all(pieces, "aux", 1, 1, tiled=True)
    mine = pieces.astype(jnp.float32).sum(1).astype(jnp.bfloat16)
    return lax.all_gather(mine, "aux", axis=1, tiled=True).astype(jnp.float32)


def aux_gather_sum(small):
    n_aux = lax.axis_size("aux")
    if n_aux & (n_aux - 1):
        return lax.all_gather(small, "aux").sum(0)
    me = lax.axis_index("aux")
    blocks = small[None]
    step = 1
    while step < n_aux:
        other = lax.ppermute(blocks, "aux", [(i, i ^ step) for i in range(n_aux)])
        blocks = jnp.where((me & step) != 0,
                           jnp.concatenate([other, blocks]), jnp.concatenate([blocks, other]))
        step *= 2
    return blocks.sum(0)


def _inverse_factor_kernel(gram_ref, inverse_ref):
    work = gram_ref[...]
    k = work.shape[0]
    rows = lax.broadcasted_iota(jnp.int32, (k, k), 0)
    lanes = lax.broadcasted_iota(jnp.int32, (k, k), 1)
    row_ids = lax.broadcasted_iota(jnp.int32, (k, 1), 0)
    lane_ids = lax.broadcasted_iota(jnp.int32, (1, k), 1)
    inverse = (rows == lanes).astype(jnp.float32)
    for j in range(k):
        pick = rows == j
        column = jnp.sum(jnp.where(lanes == j, work, 0.0), axis=1, keepdims=True)
        work_row = jnp.sum(jnp.where(pick, work, 0.0), axis=0, keepdims=True)
        inverse_row = jnp.sum(jnp.where(pick, inverse, 0.0), axis=0, keepdims=True)
        pivot = jnp.sum(jnp.where(lane_ids == j, work_row, 0.0), axis=1, keepdims=True)
        scale = 1.0 / jnp.sqrt(pivot)
        work_row = work_row * scale
        inverse_row = inverse_row * scale
        factor = jnp.where(row_ids > j, column * scale, 0.0)
        work = jnp.where(pick, work_row, work - factor * work_row)
        inverse = jnp.where(pick, inverse_row, inverse - factor * inverse_row)
    inverse_ref[...] = inverse

def inverse_factor(gram_now):
    k = gram_now.shape[0]
    return pl.pallas_call(
        _inverse_factor_kernel,
        out_shape=jax.ShapeDtypeStruct((k, k), jnp.float32),
        in_specs=[pl.BlockSpec(memory_space=pltpu.VMEM)],
        out_specs=pl.BlockSpec(memory_space=pltpu.VMEM),
    )(gram_now)


def on_device(b_tensor, eps_occ, eps_vir, trial):
    block_cols = b_tensor.shape[1]
    npair_all = eps_occ.shape[0] * eps_vir.shape[0]
    k = trial.shape[0]
    nvir = eps_vir.shape[0]
    if block_cols % nvir == 0:
        occ_rows = block_cols // nvir
        occ_block = lax.dynamic_slice_in_dim(eps_occ, lax.axis_index("pair") * occ_rows, occ_rows)
        diagonal = (eps_vir[None, :] - occ_block[:, None]).reshape(block_cols)
    else:
        everything = (eps_vir[None, :] - eps_occ[:, None]).reshape(npair_all)
        diagonal = lax.dynamic_slice_in_dim(
            everything, lax.axis_index("pair") * block_cols, block_cols)
    diag_row = diagonal[None, :]
    trial_now = trial
    for iteration in range(ITERS):
        wide_trial = trial_now.astype(jnp.float32)
        weighted = wide_trial * diag_row
        weighted_high = weighted.astype(jnp.bfloat16)
        weighted_low = (weighted - weighted_high.astype(jnp.float32)).astype(jnp.bfloat16)
        if iteration == 0:
            both = correlation_of(
                jnp.concatenate([trial_now, weighted_high, weighted_low], axis=0), trial_now, None)
            gram_part = both[:k]
            weighted_part = both[k:2 * k] + both[2 * k:]
            cross_part = correlation_of(b_tensor, trial_now, None)
        else:
            high = trial_now.astype(jnp.bfloat16)
            low = (trial_now - high.astype(jnp.float32)).astype(jnp.bfloat16)
            split = jnp.concatenate([high, low], axis=0)
            both = correlation_of(
                jnp.concatenate([high, low, weighted_high, weighted_low], axis=0), split, None)
            gram_part = both[:k, :k] + both[:k, k:] + both[k:2 * k, :k]
            weighted_part = both[2 * k:3 * k, :k] + both[2 * k:3 * k, k:] + both[3 * k:, :k]
            cross = correlation_of(b_tensor, split, None)
            cross_part = cross[:, :k] + cross[:, k:]
        summed = pair_sum(jnp.concatenate(
            [gram_part / npair_all, weighted_part / npair_all, cross_part], axis=0))
        inverse = inverse_factor(summed[:k])
        basis_now = product(inverse, wide_trial)
        projected = lax.dot_general(
            summed[2 * k:], inverse, (((1,), (1,)), ((), ())),
            precision=HIGHEST_PRECISION, preferred_element_type=jnp.float32,
        )
        group_part = lax.dot_general(
            projected, projected, (((0,), (0,)), ((), ())),
            precision=HIGHEST_PRECISION, preferred_element_type=jnp.float32,
        )
        diag_part = product(product(inverse, summed[k:2 * k]), inverse.T)
        projected_low = projected.astype(jnp.bfloat16)
        term = lax.dot_general(
            projected_low, b_tensor, (((0,), (0,)), ((), ())), preferred_element_type=jnp.float32
        ).astype(jnp.bfloat16)
        subspace = aux_gather_sum(group_part / npair_all) + diag_part
        image_now = aux_sum(term) + diag_row * basis_now
        residual = image_now - product(subspace, basis_now)
        trial_now = basis_now - residual / diag_row
    return (trial_now, residual.astype(jnp.bfloat16), subspace)


def solution(mesh):
    in_specs = (P("aux", "pair"), P(), P(), P(None, "pair"))
    out_specs = (P(None, "pair"), P(None, "pair"), P())
    return jax.shard_map(
        on_device, mesh=mesh, in_specs=in_specs, out_specs=out_specs, check_vma=False
    )
```

```python
import jax
import jax.numpy as jnp
from jax import lax
from jax.sharding import PartitionSpec as P
from jax.experimental import pallas as pl
from jax.experimental.pallas import tpu as pltpu

ITERS = 2


HIGHEST_PRECISION = lax.Precision.HIGHEST


def correlation_of(first_rows, second_rows, precision=HIGHEST_PRECISION):
    return lax.dot_general(
        first_rows,
        second_rows,
        (((1,), (1,)), ((), ())),
        precision=precision,
        preferred_element_type=jnp.float32,
    )


def product(first_mat, second_mat):
    return jnp.dot(
        first_mat, second_mat, precision=HIGHEST_PRECISION, preferred_element_type=jnp.float32
    )


def pair_sum(matrices):
    return lax.all_gather(matrices, "pair").sum(0)


def aux_sum(terms, small):
    n_aux = lax.axis_size("aux")
    rows, cols = terms.shape
    k = small.shape[0]
    upper = lax.broadcasted_iota(jnp.int32, (k, k), 1) >= lax.broadcasted_iota(jnp.int32, (k, k), 0)
    high = small.astype(jnp.bfloat16)
    low = (small - high.astype(jnp.float32)).astype(jnp.bfloat16)
    packed = jnp.where(upper, high, low.T)
    extra = jnp.concatenate([packed, jnp.diagonal(low)[:, None]], axis=1)
    pieces = jnp.concatenate([
        terms.reshape(rows, n_aux, cols // n_aux),
        jnp.broadcast_to(extra[:, None, :], (rows, n_aux, k + 1)),
    ], axis=2)
    pieces = lax.all_to_all(pieces, "aux", 1, 1, tiled=True)
    mine = pieces[:, :, : cols // n_aux].astype(jnp.float32).sum(1).astype(jnp.bfloat16)
    got = pieces[:, :, cols // n_aux:].astype(jnp.float32).sum(1)
    got_packed = got[:, :k]
    got_high = jnp.where(upper, got_packed, got_packed.T)
    got_low = jnp.where(upper, got_packed.T, got_packed)
    got_low = jnp.where(upper & upper.T, jnp.diag(got[:, k]), got_low)
    small_sum = got_high + got_low
    return lax.all_gather(mine, "aux", axis=1, tiled=True).astype(jnp.float32), small_sum


def _inverse_factor_kernel(gram_ref, inverse_ref):
    work = gram_ref[...]
    k = work.shape[0]
    rows = lax.broadcasted_iota(jnp.int32, (k, k), 0)
    lanes = lax.broadcasted_iota(jnp.int32, (k, k), 1)
    row_ids = lax.broadcasted_iota(jnp.int32, (k, 1), 0)
    lane_ids = lax.broadcasted_iota(jnp.int32, (1, k), 1)
    inverse = (rows == lanes).astype(jnp.float32)
    for j in range(k):
        pick = rows == j
        column = jnp.sum(jnp.where(lanes == j, work, 0.0), axis=1, keepdims=True)
        work_row = jnp.sum(jnp.where(pick, work, 0.0), axis=0, keepdims=True)
        inverse_row = jnp.sum(jnp.where(pick, inverse, 0.0), axis=0, keepdims=True)
        pivot = jnp.sum(jnp.where(lane_ids == j, work_row, 0.0), axis=1, keepdims=True)
        scale = 1.0 / jnp.sqrt(pivot)
        work_row = work_row * scale
        inverse_row = inverse_row * scale
        factor = jnp.where(row_ids > j, column * scale, 0.0)
        work = jnp.where(pick, work_row, work - factor * work_row)
        inverse = jnp.where(pick, inverse_row, inverse - factor * inverse_row)
    inverse_ref[...] = inverse

def inverse_factor(gram_now):
    k = gram_now.shape[0]
    return pl.pallas_call(
        _inverse_factor_kernel,
        out_shape=jax.ShapeDtypeStruct((k, k), jnp.float32),
        in_specs=[pl.BlockSpec(memory_space=pltpu.VMEM)],
        out_specs=pl.BlockSpec(memory_space=pltpu.VMEM),
    )(gram_now)


def on_device(b_tensor, eps_occ, eps_vir, trial):
    block_cols = b_tensor.shape[1]
    npair_all = eps_occ.shape[0] * eps_vir.shape[0]
    k = trial.shape[0]
    nvir = eps_vir.shape[0]
    if block_cols % nvir == 0:
        occ_rows = block_cols // nvir
        occ_block = lax.dynamic_slice_in_dim(eps_occ, lax.axis_index("pair") * occ_rows, occ_rows)
        diagonal = (eps_vir[None, :] - occ_block[:, None]).reshape(block_cols)
    else:
        everything = (eps_vir[None, :] - eps_occ[:, None]).reshape(npair_all)
        diagonal = lax.dynamic_slice_in_dim(
            everything, lax.axis_index("pair") * block_cols, block_cols)
    diag_row = diagonal[None, :]
    trial_now = trial
    for iteration in range(ITERS):
        wide_trial = trial_now.astype(jnp.float32)
        weighted = wide_trial * diag_row
        weighted_high = weighted.astype(jnp.bfloat16)
        weighted_low = (weighted - weighted_high.astype(jnp.float32)).astype(jnp.bfloat16)
        if iteration == 0:
            both = correlation_of(
                jnp.concatenate([trial_now, weighted_high, weighted_low], axis=0), trial_now, None)
            gram_part = both[:k]
            weighted_part = both[k:2 * k] + both[2 * k:]
            cross_part = correlation_of(b_tensor, trial_now, None)
        else:
            high = trial_now.astype(jnp.bfloat16)
            low = (trial_now - high.astype(jnp.float32)).astype(jnp.bfloat16)
            split = jnp.concatenate([high, low], axis=0)
            both = correlation_of(
                jnp.concatenate([high, low, weighted_high, weighted_low], axis=0), split, None)
            gram_part = both[:k, :k] + both[:k, k:] + both[k:2 * k, :k]
            weighted_part = both[2 * k:3 * k, :k] + both[2 * k:3 * k, k:] + both[3 * k:, :k]
            cross = correlation_of(b_tensor, split, None)
            cross_part = cross[:, :k] + cross[:, k:]
        summed = pair_sum(jnp.concatenate(
            [gram_part / npair_all, weighted_part / npair_all, cross_part], axis=0))
        inverse = inverse_factor(summed[:k])
        basis_now = product(inverse, wide_trial)
        projected = lax.dot_general(
            summed[2 * k:], inverse, (((1,), (1,)), ((), ())),
            precision=HIGHEST_PRECISION, preferred_element_type=jnp.float32,
        )
        group_part = lax.dot_general(
            projected, projected, (((0,), (0,)), ((), ())),
            precision=HIGHEST_PRECISION, preferred_element_type=jnp.float32,
        )
        diag_part = product(product(inverse, summed[k:2 * k]), inverse.T)
        projected_low = projected.astype(jnp.bfloat16)
        term = lax.dot_general(
            projected_low, b_tensor, (((0,), (0,)), ((), ())), preferred_element_type=jnp.float32
        ).astype(jnp.bfloat16)
        coupling, group_sum = aux_sum(term, group_part / npair_all)
        subspace = group_sum + diag_part
        image_now = coupling + diag_row * basis_now
        residual = image_now - product(subspace, basis_now)
        trial_now = basis_now - residual / diag_row
    return (trial_now, residual.astype(jnp.bfloat16), subspace)


def solution(mesh):
    in_specs = (P("aux", "pair"), P(), P(), P(None, "pair"))
    out_specs = (P(None, "pair"), P(None, "pair"), P())
    return jax.shard_map(
        on_device, mesh=mesh, in_specs=in_specs, out_specs=out_specs, check_vma=False
    )
```

```python
import jax
import jax.numpy as jnp
from jax import lax
from jax.sharding import PartitionSpec as P
from jax.experimental import pallas as pl
from jax.experimental.pallas import tpu as pltpu

ITERS = 2


HIGHEST_PRECISION = lax.Precision.HIGHEST


def correlation_of(first_rows, second_rows, precision=HIGHEST_PRECISION):
    return lax.dot_general(
        first_rows,
        second_rows,
        (((1,), (1,)), ((), ())),
        precision=precision,
        preferred_element_type=jnp.float32,
    )


def product(first_mat, second_mat):
    return jnp.dot(
        first_mat, second_mat, precision=HIGHEST_PRECISION, preferred_element_type=jnp.float32
    )


def split_product(first_mat, second_mat):
    first_high = first_mat.astype(jnp.bfloat16)
    first_low = (first_mat - first_high.astype(jnp.float32)).astype(jnp.bfloat16)
    second_high = second_mat.astype(jnp.bfloat16)
    second_low = (second_mat - second_high.astype(jnp.float32)).astype(jnp.bfloat16)
    return jnp.dot(
        jnp.concatenate([first_high, first_low, first_high], axis=1),
        jnp.concatenate([second_high, second_high, second_low], axis=0),
        preferred_element_type=jnp.float32,
    )


def pair_sum(matrices):
    return lax.all_gather(matrices, "pair").sum(0)


def aux_sum(terms, small):
    n_aux = lax.axis_size("aux")
    rows, cols = terms.shape
    high = small.astype(jnp.bfloat16)
    low = (small - high.astype(jnp.float32)).astype(jnp.bfloat16)
    extra = jnp.concatenate([high, low], axis=1)
    pieces = jnp.concatenate([
        terms.reshape(rows, n_aux, cols // n_aux),
        jnp.broadcast_to(extra[:, None, :], (rows, n_aux, extra.shape[1])),
    ], axis=2)
    pieces = lax.all_to_all(pieces, "aux", 1, 1, tiled=True)
    mine = pieces[:, :, : cols // n_aux].astype(jnp.float32).sum(1).astype(jnp.bfloat16)
    parts = pieces[:, :, cols // n_aux:].astype(jnp.float32)
    width = small.shape[1]
    small_sum = (parts[:, :, :width] + parts[:, :, width:]).sum(1)
    return lax.all_gather(mine, "aux", axis=1, tiled=True).astype(jnp.float32), small_sum


def _inverse_factor_kernel(gram_ref, inverse_ref):
    work = gram_ref[...]
    k = work.shape[0]
    rows = lax.broadcasted_iota(jnp.int32, (k, k), 0)
    lanes = lax.broadcasted_iota(jnp.int32, (k, k), 1)
    row_ids = lax.broadcasted_iota(jnp.int32, (k, 1), 0)
    lane_ids = lax.broadcasted_iota(jnp.int32, (1, k), 1)
    inverse = (rows == lanes).astype(jnp.float32)
    for j in range(k):
        pick = rows == j
        column = jnp.sum(jnp.where(lanes == j, work, 0.0), axis=1, keepdims=True)
        work_row = jnp.sum(jnp.where(pick, work, 0.0), axis=0, keepdims=True)
        inverse_row = jnp.sum(jnp.where(pick, inverse, 0.0), axis=0, keepdims=True)
        pivot = jnp.sum(jnp.where(lane_ids == j, work_row, 0.0), axis=1, keepdims=True)
        scale = 1.0 / jnp.sqrt(pivot)
        work_row = work_row * scale
        inverse_row = inverse_row * scale
        factor = jnp.where(row_ids > j, column * scale, 0.0)
        work = jnp.where(pick, work_row, work - factor * work_row)
        inverse = jnp.where(pick, inverse_row, inverse - factor * inverse_row)
    inverse_ref[...] = inverse

def inverse_factor(gram_now):
    k = gram_now.shape[0]
    return pl.pallas_call(
        _inverse_factor_kernel,
        out_shape=jax.ShapeDtypeStruct((k, k), jnp.float32),
        in_specs=[pl.BlockSpec(memory_space=pltpu.VMEM)],
        out_specs=pl.BlockSpec(memory_space=pltpu.VMEM),
    )(gram_now)


def on_device(b_tensor, eps_occ, eps_vir, trial):
    block_cols = b_tensor.shape[1]
    npair_all = eps_occ.shape[0] * eps_vir.shape[0]
    k = trial.shape[0]
    nvir = eps_vir.shape[0]
    if block_cols % nvir == 0:
        occ_rows = block_cols // nvir
        occ_block = lax.dynamic_slice_in_dim(eps_occ, lax.axis_index("pair") * occ_rows, occ_rows)
        diagonal = (eps_vir[None, :] - occ_block[:, None]).reshape(block_cols)
    else:
        everything = (eps_vir[None, :] - eps_occ[:, None]).reshape(npair_all)
        diagonal = lax.dynamic_slice_in_dim(
            everything, lax.axis_index("pair") * block_cols, block_cols)
    diag_row = diagonal[None, :]
    trial_now = trial
    for iteration in range(ITERS):
        wide_trial = trial_now.astype(jnp.float32)
        weighted = wide_trial * diag_row
        weighted_high = weighted.astype(jnp.bfloat16)
        weighted_low = (weighted - weighted_high.astype(jnp.float32)).astype(jnp.bfloat16)
        if iteration == 0:
            both = correlation_of(
                jnp.concatenate([trial_now, weighted_high, weighted_low], axis=0), trial_now, None)
            gram_part = both[:k]
            weighted_part = both[k:2 * k] + both[2 * k:]
            cross_part = correlation_of(b_tensor, trial_now, None)
        else:
            high = trial_now.astype(jnp.bfloat16)
            low = (trial_now - high.astype(jnp.float32)).astype(jnp.bfloat16)
            split = jnp.concatenate([high, low], axis=0)
            both = correlation_of(
                jnp.concatenate([high, low, weighted_high, weighted_low], axis=0), split, None)
            gram_part = both[:k, :k] + both[:k, k:] + both[k:2 * k, :k]
            weighted_part = both[2 * k:3 * k, :k] + both[2 * k:3 * k, k:] + both[3 * k:, :k]
            cross = correlation_of(b_tensor, split, None)
            cross_part = cross[:, :k] + cross[:, k:]
        summed = pair_sum(jnp.concatenate(
            [gram_part / npair_all, weighted_part / npair_all, cross_part], axis=0))
        inverse = inverse_factor(summed[:k])
        basis_now = split_product(inverse, wide_trial)
        projected = lax.dot_general(
            summed[2 * k:], inverse, (((1,), (1,)), ((), ())),
            precision=HIGHEST_PRECISION, preferred_element_type=jnp.float32,
        )
        group_part = lax.dot_general(
            projected, projected, (((0,), (0,)), ((), ())),
            precision=HIGHEST_PRECISION, preferred_element_type=jnp.float32,
        )
        diag_part = product(product(inverse, summed[k:2 * k]), inverse.T)
        projected_low = projected.astype(jnp.bfloat16)
        term = lax.dot_general(
            projected_low, b_tensor, (((0,), (0,)), ((), ())), preferred_element_type=jnp.float32
        ).astype(jnp.bfloat16)
        coupling, group_sum = aux_sum(term, group_part / npair_all)
        subspace = group_sum + diag_part
        image_now = coupling + diag_row * basis_now
        residual = image_now - split_product(subspace, basis_now)
        trial_now = basis_now - residual / diag_row
    return (trial_now, residual.astype(jnp.bfloat16), subspace)


def solution(mesh):
    in_specs = (P("aux", "pair"), P(), P(), P(None, "pair"))
    out_specs = (P(None, "pair"), P(None, "pair"), P())
    return jax.shard_map(
        on_device, mesh=mesh, in_specs=in_specs, out_specs=out_specs, check_vma=False
    )
```

```python
import jax
import jax.numpy as jnp
from jax import lax
from jax.sharding import PartitionSpec as P
from jax.experimental import pallas as pl
from jax.experimental.pallas import tpu as pltpu

ITERS = 2


HIGHEST_PRECISION = lax.Precision.HIGHEST


def correlation_of(first_rows, second_rows, precision=HIGHEST_PRECISION):
    return lax.dot_general(
        first_rows,
        second_rows,
        (((1,), (1,)), ((), ())),
        precision=precision,
        preferred_element_type=jnp.float32,
    )


def product(first_mat, second_mat):
    return jnp.dot(
        first_mat, second_mat, precision=HIGHEST_PRECISION, preferred_element_type=jnp.float32
    )


def split_product(first_mat, second_mat):
    first_high = first_mat.astype(jnp.bfloat16)
    first_low = (first_mat - first_high.astype(jnp.float32)).astype(jnp.bfloat16)
    second_high = second_mat.astype(jnp.bfloat16)
    second_low = (second_mat - second_high.astype(jnp.float32)).astype(jnp.bfloat16)
    return jnp.dot(
        jnp.concatenate([first_high, first_low, first_high], axis=1),
        jnp.concatenate([second_high, second_high, second_low], axis=0),
        preferred_element_type=jnp.float32,
    )


def pair_sum(matrices):
    return lax.all_gather(matrices, "pair").sum(0)


def aux_sum(terms, small):
    n_aux = lax.axis_size("aux")
    rows, cols = terms.shape
    high = small.astype(jnp.bfloat16)
    low = (small - high.astype(jnp.float32)).astype(jnp.bfloat16)
    extra = jnp.concatenate([high, low], axis=1)
    pieces = jnp.concatenate([
        terms.reshape(rows, n_aux, cols // n_aux),
        jnp.broadcast_to(extra[:, None, :], (rows, n_aux, extra.shape[1])),
    ], axis=2)
    pieces = lax.all_to_all(pieces, "aux", 1, 1, tiled=True)
    mine = pieces[:, :, : cols // n_aux].astype(jnp.float32).sum(1).astype(jnp.bfloat16)
    parts = pieces[:, :, cols // n_aux:].astype(jnp.float32)
    width = small.shape[1]
    small_sum = (parts[:, :, :width] + parts[:, :, width:]).sum(1)
    return lax.all_gather(mine, "aux", axis=1, tiled=True).astype(jnp.float32), small_sum


def _inverse_factor_kernel(gram_ref, inverse_ref):
    work = gram_ref[...]
    k = work.shape[0]
    rows = lax.broadcasted_iota(jnp.int32, (k, k), 0)
    lanes = lax.broadcasted_iota(jnp.int32, (k, k), 1)
    row_ids = lax.broadcasted_iota(jnp.int32, (k, 1), 0)
    lane_ids = lax.broadcasted_iota(jnp.int32, (1, k), 1)
    inverse = (rows == lanes).astype(jnp.float32)
    for j in range(k):
        pick = rows == j
        column = jnp.sum(jnp.where(lanes == j, work, 0.0), axis=1, keepdims=True)
        work_row = jnp.sum(jnp.where(pick, work, 0.0), axis=0, keepdims=True)
        inverse_row = jnp.sum(jnp.where(pick, inverse, 0.0), axis=0, keepdims=True)
        pivot = jnp.sum(jnp.where(lane_ids == j, work_row, 0.0), axis=1, keepdims=True)
        scale = 1.0 / jnp.sqrt(pivot)
        work_row = work_row * scale
        inverse_row = inverse_row * scale
        factor = jnp.where(row_ids > j, column * scale, 0.0)
        work = jnp.where(pick, work_row, work - factor * work_row)
        inverse = jnp.where(pick, inverse_row, inverse - factor * inverse_row)
    inverse_ref[...] = inverse

def inverse_factor(gram_now):
    k = gram_now.shape[0]
    return pl.pallas_call(
        _inverse_factor_kernel,
        out_shape=jax.ShapeDtypeStruct((k, k), jnp.float32),
        in_specs=[pl.BlockSpec(memory_space=pltpu.VMEM)],
        out_specs=pl.BlockSpec(memory_space=pltpu.VMEM),
    )(gram_now)


def on_device(b_tensor, eps_occ, eps_vir, trial):
    block_cols = b_tensor.shape[1]
    npair_all = eps_occ.shape[0] * eps_vir.shape[0]
    k = trial.shape[0]
    nvir = eps_vir.shape[0]
    if block_cols % nvir == 0:
        occ_rows = block_cols // nvir
        occ_block = lax.dynamic_slice_in_dim(eps_occ, lax.axis_index("pair") * occ_rows, occ_rows)
        diagonal = (eps_vir[None, :] - occ_block[:, None]).reshape(block_cols)
    else:
        everything = (eps_vir[None, :] - eps_occ[:, None]).reshape(npair_all)
        diagonal = lax.dynamic_slice_in_dim(
            everything, lax.axis_index("pair") * block_cols, block_cols)
    diag_row = diagonal[None, :]
    trial_now = trial
    for iteration in range(ITERS):
        wide_trial = trial_now.astype(jnp.float32)
        weighted = wide_trial * diag_row
        weighted_high = weighted.astype(jnp.bfloat16)
        weighted_low = (weighted - weighted_high.astype(jnp.float32)).astype(jnp.bfloat16)
        if iteration == 0:
            both = correlation_of(
                jnp.concatenate([trial_now, weighted_high, weighted_low], axis=0), trial_now, None)
            gram_part = both[:k]
            weighted_part = both[k:2 * k] + both[2 * k:]
            cross_part = correlation_of(b_tensor, trial_now, None)
        else:
            high = trial_now.astype(jnp.bfloat16)
            low = (trial_now - high.astype(jnp.float32)).astype(jnp.bfloat16)
            split = jnp.concatenate([high, low], axis=0)
            both = correlation_of(
                jnp.concatenate([high, low, weighted_high, weighted_low], axis=0), split, None)
            gram_part = both[:k, :k] + both[:k, k:] + both[k:2 * k, :k]
            weighted_part = both[2 * k:3 * k, :k] + both[2 * k:3 * k, k:] + both[3 * k:, :k]
            cross = correlation_of(b_tensor, split, None)
            cross_part = cross[:, :k] + cross[:, k:]
        summed = pair_sum(jnp.concatenate(
            [gram_part / npair_all, weighted_part / npair_all, cross_part], axis=0))
        inverse = inverse_factor(summed[:k])
        basis_now = product(inverse, wide_trial)
        projected = lax.dot_general(
            summed[2 * k:], inverse, (((1,), (1,)), ((), ())),
            precision=HIGHEST_PRECISION, preferred_element_type=jnp.float32,
        )
        group_part = lax.dot_general(
            projected, projected, (((0,), (0,)), ((), ())),
            precision=HIGHEST_PRECISION, preferred_element_type=jnp.float32,
        )
        diag_part = product(product(inverse, summed[k:2 * k]), inverse.T)
        projected_low = projected.astype(jnp.bfloat16)
        term = lax.dot_general(
            projected_low, b_tensor, (((0,), (0,)), ((), ())), preferred_element_type=jnp.float32
        ).astype(jnp.bfloat16)
        coupling, group_sum = aux_sum(term, group_part / npair_all)
        subspace = group_sum + diag_part
        image_now = coupling + diag_row * basis_now
        residual = image_now - split_product(subspace, basis_now)
        trial_now = basis_now - residual / diag_row
    return (trial_now, residual.astype(jnp.bfloat16), subspace)


def solution(mesh):
    in_specs = (P("aux", "pair"), P(), P(), P(None, "pair"))
    out_specs = (P(None, "pair"), P(None, "pair"), P())
    return jax.shard_map(
        on_device, mesh=mesh, in_specs=in_specs, out_specs=out_specs, check_vma=False
    )
```

```python
import jax
import jax.numpy as jnp
from jax import lax
from jax.sharding import PartitionSpec as P
from jax.experimental import pallas as pl
from jax.experimental.pallas import tpu as pltpu

ITERS = 2


HIGHEST_PRECISION = lax.Precision.HIGHEST


def correlation_of(first_rows, second_rows, precision=HIGHEST_PRECISION):
    return lax.dot_general(
        first_rows,
        second_rows,
        (((1,), (1,)), ((), ())),
        precision=precision,
        preferred_element_type=jnp.float32,
    )


def product(first_mat, second_mat):
    return jnp.dot(
        first_mat, second_mat, precision=HIGHEST_PRECISION, preferred_element_type=jnp.float32
    )


def split_bf16(values):
    high_wide = lax.reduce_precision(values, exponent_bits=8, mantissa_bits=7)
    return high_wide.astype(jnp.bfloat16), (values - high_wide).astype(jnp.bfloat16)


def split_product(first_mat, second_mat):
    first_high, first_low = split_bf16(first_mat)
    second_high, second_low = split_bf16(second_mat)
    return jnp.dot(
        jnp.concatenate([first_high, first_low, first_high], axis=1),
        jnp.concatenate([second_high, second_high, second_low], axis=0),
        preferred_element_type=jnp.float32,
    )


def pair_sum(matrices):
    return lax.all_gather(matrices, "pair").sum(0)


def aux_sum(terms, small):
    n_aux = lax.axis_size("aux")
    rows, cols = terms.shape
    high, low = split_bf16(small)
    extra = jnp.concatenate([high, low], axis=1)
    pieces = jnp.concatenate([
        terms.reshape(rows, n_aux, cols // n_aux),
        jnp.broadcast_to(extra[:, None, :], (rows, n_aux, extra.shape[1])),
    ], axis=2)
    pieces = lax.all_to_all(pieces, "aux", 1, 1, tiled=True)
    mine = pieces[:, :, : cols // n_aux].astype(jnp.float32).sum(1).astype(jnp.bfloat16)
    parts = pieces[:, :, cols // n_aux:].astype(jnp.float32)
    width = small.shape[1]
    small_sum = (parts[:, :, :width] + parts[:, :, width:]).sum(1)
    return lax.all_gather(mine, "aux", axis=1, tiled=True).astype(jnp.float32), small_sum


def _inverse_factor_kernel(gram_ref, inverse_ref):
    work = gram_ref[...]
    k = work.shape[0]
    rows = lax.broadcasted_iota(jnp.int32, (k, k), 0)
    lanes = lax.broadcasted_iota(jnp.int32, (k, k), 1)
    row_ids = lax.broadcasted_iota(jnp.int32, (k, 1), 0)
    lane_ids = lax.broadcasted_iota(jnp.int32, (1, k), 1)
    inverse = (rows == lanes).astype(jnp.float32)
    for j in range(k):
        pick = rows == j
        column = jnp.sum(jnp.where(lanes == j, work, 0.0), axis=1, keepdims=True)
        work_row = jnp.sum(jnp.where(pick, work, 0.0), axis=0, keepdims=True)
        inverse_row = jnp.sum(jnp.where(pick, inverse, 0.0), axis=0, keepdims=True)
        pivot = jnp.sum(jnp.where(lane_ids == j, work_row, 0.0), axis=1, keepdims=True)
        scale = 1.0 / jnp.sqrt(pivot)
        work_row = work_row * scale
        inverse_row = inverse_row * scale
        factor = jnp.where(row_ids > j, column * scale, 0.0)
        work = jnp.where(pick, work_row, work - factor * work_row)
        inverse = jnp.where(pick, inverse_row, inverse - factor * inverse_row)
    inverse_ref[...] = inverse

def inverse_factor(gram_now):
    k = gram_now.shape[0]
    return pl.pallas_call(
        _inverse_factor_kernel,
        out_shape=jax.ShapeDtypeStruct((k, k), jnp.float32),
        in_specs=[pl.BlockSpec(memory_space=pltpu.VMEM)],
        out_specs=pl.BlockSpec(memory_space=pltpu.VMEM),
    )(gram_now)


def on_device(b_tensor, eps_occ, eps_vir, trial):
    block_cols = b_tensor.shape[1]
    npair_all = eps_occ.shape[0] * eps_vir.shape[0]
    k = trial.shape[0]
    nvir = eps_vir.shape[0]
    if block_cols % nvir == 0:
        occ_rows = block_cols // nvir
        occ_block = lax.dynamic_slice_in_dim(eps_occ, lax.axis_index("pair") * occ_rows, occ_rows)
        diagonal = (eps_vir[None, :] - occ_block[:, None]).reshape(block_cols)
    else:
        everything = (eps_vir[None, :] - eps_occ[:, None]).reshape(npair_all)
        diagonal = lax.dynamic_slice_in_dim(
            everything, lax.axis_index("pair") * block_cols, block_cols)
    diag_row = diagonal[None, :]
    trial_now = trial
    for iteration in range(ITERS):
        wide_trial = trial_now.astype(jnp.float32)
        weighted = wide_trial * diag_row
        weighted_high, weighted_low = split_bf16(weighted)
        if iteration == 0:
            both = correlation_of(
                jnp.concatenate([trial_now, weighted_high, weighted_low], axis=0), trial_now, None)
            gram_part = both[:k]
            weighted_part = both[k:2 * k] + both[2 * k:]
            cross_part = correlation_of(b_tensor, trial_now, None)
        else:
            high, low = split_bf16(trial_now)
            split = jnp.concatenate([high, low], axis=0)
            both = correlation_of(
                jnp.concatenate([high, low, weighted_high, weighted_low], axis=0), split, None)
            gram_part = both[:k, :k] + both[:k, k:] + both[k:2 * k, :k]
            weighted_part = both[2 * k:3 * k, :k] + both[2 * k:3 * k, k:] + both[3 * k:, :k]
            cross = correlation_of(b_tensor, split, None)
            cross_part = cross[:, :k] + cross[:, k:]
        summed = pair_sum(jnp.concatenate(
            [gram_part / npair_all, weighted_part / npair_all, cross_part], axis=0))
        inverse = inverse_factor(summed[:k])
        basis_now = split_product(inverse, wide_trial)
        projected = lax.dot_general(
            summed[2 * k:], inverse, (((1,), (1,)), ((), ())),
            precision=HIGHEST_PRECISION, preferred_element_type=jnp.float32,
        )
        group_part = lax.dot_general(
            projected, projected, (((0,), (0,)), ((), ())),
            precision=HIGHEST_PRECISION, preferred_element_type=jnp.float32,
        )
        diag_part = product(product(inverse, summed[k:2 * k]), inverse.T)
        projected_low = projected.astype(jnp.bfloat16)
        term = lax.dot_general(
            projected_low, b_tensor, (((0,), (0,)), ((), ())), preferred_element_type=jnp.float32
        ).astype(jnp.bfloat16)
        coupling, group_sum = aux_sum(term, group_part / npair_all)
        subspace = group_sum + diag_part
        image_now = coupling + diag_row * basis_now
        residual = image_now - split_product(subspace, basis_now)
        trial_now = basis_now - residual / diag_row
    return (trial_now, residual.astype(jnp.bfloat16), subspace)


def solution(mesh):
    in_specs = (P("aux", "pair"), P(), P(), P(None, "pair"))
    out_specs = (P(None, "pair"), P(None, "pair"), P())
    return jax.shard_map(
        on_device, mesh=mesh, in_specs=in_specs, out_specs=out_specs, check_vma=False
    )
```

```python
import jax
import jax.numpy as jnp
from jax import lax
from jax.sharding import PartitionSpec as P
from jax.experimental import pallas as pl
from jax.experimental.pallas import tpu as pltpu

ITERS = 2


HIGHEST_PRECISION = lax.Precision.HIGHEST


def correlation_of(first_rows, second_rows, precision=HIGHEST_PRECISION):
    return lax.dot_general(
        first_rows,
        second_rows,
        (((1,), (1,)), ((), ())),
        precision=precision,
        preferred_element_type=jnp.float32,
    )


def product(first_mat, second_mat):
    return jnp.dot(
        first_mat, second_mat, precision=HIGHEST_PRECISION, preferred_element_type=jnp.float32
    )


def split_bf16(values):
    high_wide = lax.reduce_precision(values, exponent_bits=8, mantissa_bits=7)
    return high_wide.astype(jnp.bfloat16), (values - high_wide).astype(jnp.bfloat16)


def split_product(first_mat, second_mat):
    first_high, first_low = split_bf16(first_mat)
    second_high, second_low = split_bf16(second_mat)
    return jnp.dot(
        jnp.concatenate([first_high, first_low, first_high], axis=1),
        jnp.concatenate([second_high, second_high, second_low], axis=0),
        preferred_element_type=jnp.float32,
    )


def pair_sum(matrices):
    return lax.all_gather(matrices, "pair").sum(0)


def aux_sum(terms, small):
    n_aux = lax.axis_size("aux")
    rows, cols = terms.shape
    high, low = split_bf16(small)
    extra = jnp.concatenate([high, low], axis=1)
    pieces = jnp.concatenate([
        terms.reshape(rows, n_aux, cols // n_aux),
        jnp.broadcast_to(extra[:, None, :], (rows, n_aux, extra.shape[1])),
    ], axis=2)
    pieces = lax.all_to_all(pieces, "aux", 1, 1, tiled=True)
    mine = pieces[:, :, : cols // n_aux].astype(jnp.float32).sum(1).astype(jnp.bfloat16)
    parts = pieces[:, :, cols // n_aux:].astype(jnp.float32)
    width = small.shape[1]
    small_sum = (parts[:, :, :width] + parts[:, :, width:]).sum(1)
    return lax.all_gather(mine, "aux", axis=1, tiled=True).astype(jnp.float32), small_sum


def _inverse_factor_kernel(gram_ref, inverse_ref):
    work = gram_ref[...]
    k = work.shape[0]
    rows = lax.broadcasted_iota(jnp.int32, (k, k), 0)
    lanes = lax.broadcasted_iota(jnp.int32, (k, k), 1)
    row_ids = lax.broadcasted_iota(jnp.int32, (k, 1), 0)
    inverse = (rows == lanes).astype(jnp.float32)
    for j in range(k):
        pick = rows == j
        column = jnp.sum(jnp.where(lanes == j, work, 0.0), axis=1, keepdims=True)
        work_row = jnp.sum(jnp.where(pick, work, 0.0), axis=0, keepdims=True)
        inverse_row = jnp.sum(jnp.where(pick, inverse, 0.0), axis=0, keepdims=True)
        pivot = jnp.sum(jnp.where(row_ids == j, column, 0.0), axis=0, keepdims=True)
        scale = 1.0 / jnp.sqrt(pivot)
        work_row = work_row * scale
        inverse_row = inverse_row * scale
        factor = jnp.where(row_ids > j, column * scale, 0.0)
        work = jnp.where(pick, work_row, work - factor * work_row)
        inverse = jnp.where(pick, inverse_row, inverse - factor * inverse_row)
    inverse_ref[...] = inverse

def inverse_factor(gram_now):
    k = gram_now.shape[0]
    return pl.pallas_call(
        _inverse_factor_kernel,
        out_shape=jax.ShapeDtypeStruct((k, k), jnp.float32),
        in_specs=[pl.BlockSpec(memory_space=pltpu.VMEM)],
        out_specs=pl.BlockSpec(memory_space=pltpu.VMEM),
    )(gram_now)


def on_device(b_tensor, eps_occ, eps_vir, trial):
    block_cols = b_tensor.shape[1]
    npair_all = eps_occ.shape[0] * eps_vir.shape[0]
    k = trial.shape[0]
    nvir = eps_vir.shape[0]
    if block_cols % nvir == 0:
        occ_rows = block_cols // nvir
        occ_block = lax.dynamic_slice_in_dim(eps_occ, lax.axis_index("pair") * occ_rows, occ_rows)
        diagonal = (eps_vir[None, :] - occ_block[:, None]).reshape(block_cols)
    else:
        everything = (eps_vir[None, :] - eps_occ[:, None]).reshape(npair_all)
        diagonal = lax.dynamic_slice_in_dim(
            everything, lax.axis_index("pair") * block_cols, block_cols)
    diag_row = diagonal[None, :]
    trial_now = trial
    for iteration in range(ITERS):
        wide_trial = trial_now.astype(jnp.float32)
        weighted = wide_trial * diag_row
        weighted_high, weighted_low = split_bf16(weighted)
        if iteration == 0:
            both = correlation_of(
                jnp.concatenate([trial_now, weighted_high, weighted_low], axis=0), trial_now, None)
            gram_part = both[:k]
            weighted_part = both[k:2 * k] + both[2 * k:]
            cross_part = correlation_of(b_tensor, trial_now, None)
        else:
            high, low = split_bf16(trial_now)
            split = jnp.concatenate([high, low], axis=0)
            both = correlation_of(
                jnp.concatenate([high, low, weighted_high, weighted_low], axis=0), split, None)
            gram_part = both[:k, :k] + both[:k, k:] + both[k:2 * k, :k]
            weighted_part = both[2 * k:3 * k, :k] + both[2 * k:3 * k, k:] + both[3 * k:, :k]
            cross = correlation_of(b_tensor, split, None)
            cross_part = cross[:, :k] + cross[:, k:]
        summed = pair_sum(jnp.concatenate(
            [gram_part / npair_all, weighted_part / npair_all, cross_part], axis=0))
        inverse = inverse_factor(summed[:k])
        basis_now = split_product(inverse, wide_trial)
        projected = lax.dot_general(
            summed[2 * k:], inverse, (((1,), (1,)), ((), ())),
            precision=HIGHEST_PRECISION, preferred_element_type=jnp.float32,
        )
        group_part = lax.dot_general(
            projected, projected, (((0,), (0,)), ((), ())),
            precision=HIGHEST_PRECISION, preferred_element_type=jnp.float32,
        )
        diag_part = product(product(inverse, summed[k:2 * k]), inverse.T)
        projected_low = projected.astype(jnp.bfloat16)
        term = lax.dot_general(
            projected_low, b_tensor, (((0,), (0,)), ((), ())), preferred_element_type=jnp.float32
        ).astype(jnp.bfloat16)
        coupling, group_sum = aux_sum(term, group_part / npair_all)
        subspace = group_sum + diag_part
        image_now = coupling + diag_row * basis_now
        residual = image_now - split_product(subspace, basis_now)
        trial_now = basis_now - residual / diag_row
    return (trial_now, residual.astype(jnp.bfloat16), subspace)


def solution(mesh):
    in_specs = (P("aux", "pair"), P(), P(), P(None, "pair"))
    out_specs = (P(None, "pair"), P(None, "pair"), P())
    return jax.shard_map(
        on_device, mesh=mesh, in_specs=in_specs, out_specs=out_specs, check_vma=False
    )
```

```python
import jax
import jax.numpy as jnp
from jax import lax
from jax.sharding import PartitionSpec as P
from jax.experimental import pallas as pl
from jax.experimental.pallas import tpu as pltpu

ITERS = 2


HIGHEST_PRECISION = lax.Precision.HIGHEST


def correlation_of(first_rows, second_rows, precision=HIGHEST_PRECISION):
    return lax.dot_general(
        first_rows,
        second_rows,
        (((1,), (1,)), ((), ())),
        precision=precision,
        preferred_element_type=jnp.float32,
    )


def product(first_mat, second_mat):
    return jnp.dot(
        first_mat, second_mat, precision=HIGHEST_PRECISION, preferred_element_type=jnp.float32
    )


def split_bf16(values):
    high_wide = lax.reduce_precision(values, exponent_bits=8, mantissa_bits=7)
    return high_wide.astype(jnp.bfloat16), (values - high_wide).astype(jnp.bfloat16)


def split_product(first_mat, second_mat):
    first_high, first_low = split_bf16(first_mat)
    second_high, second_low = split_bf16(second_mat)
    return jnp.dot(
        jnp.concatenate([first_high, first_low, first_high], axis=1),
        jnp.concatenate([second_high, second_high, second_low], axis=0),
        preferred_element_type=jnp.float32,
    )


def pair_sum(matrices):
    return lax.all_gather(matrices, "pair").sum(0)


def aux_sum(terms, small):
    n_aux = lax.axis_size("aux")
    rows, cols = terms.shape
    high, low = split_bf16(small)
    extra = jnp.concatenate([high, low], axis=1)
    pieces = jnp.concatenate([
        terms.reshape(rows, n_aux, cols // n_aux),
        jnp.broadcast_to(extra[:, None, :], (rows, n_aux, extra.shape[1])),
    ], axis=2)
    pieces = lax.all_to_all(pieces, "aux", 1, 1, tiled=True)
    mine = pieces[:, :, : cols // n_aux].astype(jnp.float32).sum(1).astype(jnp.bfloat16)
    parts = pieces[:, :, cols // n_aux:].astype(jnp.float32)
    width = small.shape[1]
    small_sum = (parts[:, :, :width] + parts[:, :, width:]).sum(1)
    return lax.all_gather(mine, "aux", axis=1, tiled=True).astype(jnp.float32), small_sum


def _inverse_factor_kernel(gram_ref, inverse_ref):
    work = gram_ref[...]
    k = work.shape[0]
    rows = lax.broadcasted_iota(jnp.int32, (k, k), 0)
    lanes = lax.broadcasted_iota(jnp.int32, (k, k), 1)
    row_ids = lax.broadcasted_iota(jnp.int32, (k, 1), 0)
    inverse = (rows == lanes).astype(jnp.float32)
    for j in range(k):
        pick = rows == j
        column = jnp.sum(jnp.where(lanes == j, work, 0.0), axis=1, keepdims=True)
        work_row = jnp.sum(jnp.where(pick, work, 0.0), axis=0, keepdims=True)
        inverse_row = jnp.sum(jnp.where(pick, inverse, 0.0), axis=0, keepdims=True)
        pivot = jnp.sum(jnp.where(row_ids == j, column, 0.0), axis=0, keepdims=True)
        scale = 1.0 / jnp.sqrt(pivot)
        work_row = work_row * scale
        inverse_row = inverse_row * scale
        factor = jnp.where(row_ids > j, column * scale, 0.0)
        work = jnp.where(pick, work_row, work - factor * work_row)
        inverse = jnp.where(pick, inverse_row, inverse - factor * inverse_row)
    inverse_ref[...] = inverse

def inverse_factor(gram_now):
    k = gram_now.shape[0]
    return pl.pallas_call(
        _inverse_factor_kernel,
        out_shape=jax.ShapeDtypeStruct((k, k), jnp.float32),
        in_specs=[pl.BlockSpec(memory_space=pltpu.VMEM)],
        out_specs=pl.BlockSpec(memory_space=pltpu.VMEM),
    )(gram_now)


def on_device(b_tensor, eps_occ, eps_vir, trial):
    block_cols = b_tensor.shape[1]
    npair_all = eps_occ.shape[0] * eps_vir.shape[0]
    k = trial.shape[0]
    nvir = eps_vir.shape[0]
    if block_cols % nvir == 0:
        occ_rows = block_cols // nvir
        occ_block = lax.dynamic_slice_in_dim(eps_occ, lax.axis_index("pair") * occ_rows, occ_rows)
        diagonal = (eps_vir[None, :] - occ_block[:, None]).reshape(block_cols)
    else:
        everything = (eps_vir[None, :] - eps_occ[:, None]).reshape(npair_all)
        diagonal = lax.dynamic_slice_in_dim(
            everything, lax.axis_index("pair") * block_cols, block_cols)
    diag_row = diagonal[None, :]
    inverse_diag = (1.0 / diagonal)[None, :]
    trial_now = trial
    for iteration in range(ITERS):
        wide_trial = trial_now.astype(jnp.float32)
        weighted = wide_trial * diag_row
        weighted_high, weighted_low = split_bf16(weighted)
        if iteration == 0:
            both = correlation_of(
                jnp.concatenate([trial_now, weighted_high, weighted_low], axis=0), trial_now, None)
            gram_part = both[:k]
            weighted_part = both[k:2 * k] + both[2 * k:]
            cross_part = correlation_of(b_tensor, trial_now, None)
        else:
            high, low = split_bf16(trial_now)
            split = jnp.concatenate([high, low], axis=0)
            both = correlation_of(
                jnp.concatenate([high, low, weighted_high, weighted_low], axis=0), split, None)
            gram_part = both[:k, :k] + both[:k, k:] + both[k:2 * k, :k]
            weighted_part = both[2 * k:3 * k, :k] + both[2 * k:3 * k, k:] + both[3 * k:, :k]
            cross = correlation_of(b_tensor, split, None)
            cross_part = cross[:, :k] + cross[:, k:]
        summed = pair_sum(jnp.concatenate(
            [gram_part / npair_all, weighted_part / npair_all, cross_part], axis=0))
        inverse = inverse_factor(summed[:k])
        basis_now = split_product(inverse, wide_trial)
        projected = lax.dot_general(
            summed[2 * k:], inverse, (((1,), (1,)), ((), ())),
            precision=HIGHEST_PRECISION, preferred_element_type=jnp.float32,
        )
        group_part = lax.dot_general(
            projected, projected, (((0,), (0,)), ((), ())),
            precision=HIGHEST_PRECISION, preferred_element_type=jnp.float32,
        )
        diag_part = product(product(inverse, summed[k:2 * k]), inverse.T)
        projected_low = projected.astype(jnp.bfloat16)
        term = lax.dot_general(
            projected_low, b_tensor, (((0,), (0,)), ((), ())), preferred_element_type=jnp.float32
        ).astype(jnp.bfloat16)
        coupling, group_sum = aux_sum(term, group_part / npair_all)
        subspace = group_sum + diag_part
        image_now = coupling + diag_row * basis_now
        residual = image_now - split_product(subspace, basis_now)
        trial_now = basis_now - residual * inverse_diag
    return (trial_now, residual.astype(jnp.bfloat16), subspace)


def solution(mesh):
    in_specs = (P("aux", "pair"), P(), P(), P(None, "pair"))
    out_specs = (P(None, "pair"), P(None, "pair"), P())
    return jax.shard_map(
        on_device, mesh=mesh, in_specs=in_specs, out_specs=out_specs, check_vma=False
    )
```

```python
import jax
import jax.numpy as jnp
from jax import lax
from jax.sharding import PartitionSpec as P
from jax.experimental import pallas as pl
from jax.experimental.pallas import tpu as pltpu

ITERS = 2


HIGHEST_PRECISION = lax.Precision.HIGHEST


def correlation_of(first_rows, second_rows, precision=HIGHEST_PRECISION):
    return lax.dot_general(
        first_rows,
        second_rows,
        (((1,), (1,)), ((), ())),
        precision=precision,
        preferred_element_type=jnp.float32,
    )


def product(first_mat, second_mat):
    return jnp.dot(
        first_mat, second_mat, precision=HIGHEST_PRECISION, preferred_element_type=jnp.float32
    )


def split_bf16(values):
    high_wide = lax.reduce_precision(values, exponent_bits=8, mantissa_bits=7)
    return high_wide.astype(jnp.bfloat16), (values - high_wide).astype(jnp.bfloat16)


def split_product(first_mat, second_mat):
    first_high, first_low = split_bf16(first_mat)
    second_high, second_low = split_bf16(second_mat)
    return jnp.dot(
        jnp.concatenate([first_high, first_low, first_high], axis=1),
        jnp.concatenate([second_high, second_high, second_low], axis=0),
        preferred_element_type=jnp.float32,
    )


def pair_sum(matrices):
    return lax.all_gather(matrices, "pair").sum(0)


def aux_sum(terms, small):
    n_aux = lax.axis_size("aux")
    rows, cols = terms.shape
    high, low = split_bf16(small)
    extra = jnp.concatenate([high, low], axis=1)
    pieces = jnp.concatenate([
        terms.reshape(rows, n_aux, cols // n_aux),
        jnp.broadcast_to(extra[:, None, :], (rows, n_aux, extra.shape[1])),
    ], axis=2)
    pieces = lax.all_to_all(pieces, "aux", 1, 1, tiled=True)
    mine = pieces[:, :, : cols // n_aux].astype(jnp.float32).sum(1).astype(jnp.bfloat16)
    parts = pieces[:, :, cols // n_aux:].astype(jnp.float32)
    width = small.shape[1]
    small_sum = (parts[:, :, :width] + parts[:, :, width:]).sum(1)
    return lax.all_gather(mine, "aux", axis=1, tiled=True).astype(jnp.float32), small_sum


def _inverse_factor_kernel(gram_ref, inverse_ref):
    work = gram_ref[...]
    k = work.shape[0]
    rows = lax.broadcasted_iota(jnp.int32, (k, k), 0)
    lanes = lax.broadcasted_iota(jnp.int32, (k, k), 1)
    row_ids = lax.broadcasted_iota(jnp.int32, (k, 1), 0)
    inverse = (rows == lanes).astype(jnp.float32)
    for j in range(k):
        pick = rows == j
        column = jnp.sum(jnp.where(lanes == j, work, 0.0), axis=1, keepdims=True)
        work_row = jnp.sum(jnp.where(pick, work, 0.0), axis=0, keepdims=True)
        inverse_row = jnp.sum(jnp.where(pick, inverse, 0.0), axis=0, keepdims=True)
        pivot = jnp.sum(jnp.where(row_ids == j, column, 0.0), axis=0, keepdims=True)
        scale = 1.0 / jnp.sqrt(pivot)
        work_row = work_row * scale
        inverse_row = inverse_row * scale
        factor = jnp.where(row_ids > j, column * scale, 0.0)
        work = jnp.where(pick, work_row, work - factor * work_row)
        inverse = jnp.where(pick, inverse_row, inverse - factor * inverse_row)
    inverse_ref[...] = inverse

def inverse_factor(gram_now):
    k = gram_now.shape[0]
    return pl.pallas_call(
        _inverse_factor_kernel,
        out_shape=jax.ShapeDtypeStruct((k, k), jnp.float32),
        in_specs=[pl.BlockSpec(memory_space=pltpu.VMEM)],
        out_specs=pl.BlockSpec(memory_space=pltpu.VMEM),
    )(gram_now)


def on_device(b_tensor, eps_occ, eps_vir, trial):
    block_cols = b_tensor.shape[1]
    npair_all = eps_occ.shape[0] * eps_vir.shape[0]
    k = trial.shape[0]
    nvir = eps_vir.shape[0]
    if block_cols % nvir == 0:
        occ_rows = block_cols // nvir
        occ_block = lax.dynamic_slice_in_dim(eps_occ, lax.axis_index("pair") * occ_rows, occ_rows)
        diagonal = (eps_vir[None, :] - occ_block[:, None]).reshape(block_cols)
    else:
        everything = (eps_vir[None, :] - eps_occ[:, None]).reshape(npair_all)
        diagonal = lax.dynamic_slice_in_dim(
            everything, lax.axis_index("pair") * block_cols, block_cols)
    diag_row = diagonal[None, :]
    trial_now = trial
    for iteration in range(ITERS):
        wide_trial = trial_now.astype(jnp.float32)
        weighted = wide_trial * diag_row
        weighted_high, weighted_low = split_bf16(weighted)
        if iteration == 0:
            both = correlation_of(
                jnp.concatenate([trial_now, weighted_high, weighted_low], axis=0), trial_now, None)
            gram_part = both[:k]
            weighted_part = both[k:2 * k] + both[2 * k:]
            cross_part = correlation_of(b_tensor, trial_now, None)
        else:
            high, low = split_bf16(trial_now)
            split = jnp.concatenate([high, low], axis=0)
            both = correlation_of(
                jnp.concatenate([high, low, weighted_high, weighted_low], axis=0), split, None)
            gram_part = both[:k, :k] + both[:k, k:] + both[k:2 * k, :k]
            weighted_part = both[2 * k:3 * k, :k] + both[2 * k:3 * k, k:] + both[3 * k:, :k]
            cross = correlation_of(b_tensor, split, None)
            cross_part = cross[:, :k] + cross[:, k:]
        summed = pair_sum(jnp.concatenate(
            [gram_part / npair_all, weighted_part / npair_all, cross_part], axis=0))
        inverse = inverse_factor(summed[:k].T)
        basis_now = split_product(inverse, wide_trial)
        projected = lax.dot_general(
            summed[2 * k:], inverse, (((1,), (1,)), ((), ())),
            precision=HIGHEST_PRECISION, preferred_element_type=jnp.float32,
        )
        group_part = lax.dot_general(
            projected, projected, (((0,), (0,)), ((), ())),
            precision=HIGHEST_PRECISION, preferred_element_type=jnp.float32,
        )
        diag_part = product(product(inverse, summed[k:2 * k]), inverse.T)
        projected_low = projected.astype(jnp.bfloat16)
        term = lax.dot_general(
            projected_low, b_tensor, (((0,), (0,)), ((), ())), preferred_element_type=jnp.float32
        ).astype(jnp.bfloat16)
        coupling, group_sum = aux_sum(term, group_part / npair_all)
        subspace = group_sum + diag_part
        image_now = coupling + diag_row * basis_now
        residual = image_now - split_product(subspace, basis_now)
        trial_now = basis_now - residual / diag_row
    return (trial_now, residual.astype(jnp.bfloat16), subspace)


def solution(mesh):
    in_specs = (P("aux", "pair"), P(), P(), P(None, "pair"))
    out_specs = (P(None, "pair"), P(None, "pair"), P())
    return jax.shard_map(
        on_device, mesh=mesh, in_specs=in_specs, out_specs=out_specs, check_vma=False
    )
```

```python
import jax
import jax.numpy as jnp
from jax import lax
from jax.sharding import PartitionSpec as P
from jax.experimental import pallas as pl
from jax.experimental.pallas import tpu as pltpu

ITERS = 2


HIGHEST_PRECISION = lax.Precision.HIGHEST


def correlation_of(first_rows, second_rows, precision=HIGHEST_PRECISION):
    return lax.dot_general(
        first_rows,
        second_rows,
        (((1,), (1,)), ((), ())),
        precision=precision,
        preferred_element_type=jnp.float32,
    )


def product(first_mat, second_mat):
    return jnp.dot(
        first_mat, second_mat, precision=HIGHEST_PRECISION, preferred_element_type=jnp.float32
    )


def split_bf16(values):
    high_wide = lax.reduce_precision(values, exponent_bits=8, mantissa_bits=7)
    return high_wide.astype(jnp.bfloat16), (values - high_wide).astype(jnp.bfloat16)


def split_product(first_mat, second_mat):
    first_high, first_low = split_bf16(first_mat)
    second_high, second_low = split_bf16(second_mat)
    return jnp.dot(
        jnp.concatenate([first_high, first_low, first_high], axis=1),
        jnp.concatenate([second_high, second_high, second_low], axis=0),
        preferred_element_type=jnp.float32,
    )


def pair_sum(matrices):
    return lax.all_gather(matrices, "pair").sum(0)


def aux_sum(terms, small):
    n_aux = lax.axis_size("aux")
    rows, cols = terms.shape
    high, low = split_bf16(small)
    extra = jnp.concatenate([high, low], axis=1)
    pieces = jnp.concatenate([
        terms.reshape(rows, n_aux, cols // n_aux),
        jnp.broadcast_to(extra[:, None, :], (rows, n_aux, extra.shape[1])),
    ], axis=2)
    pieces = lax.all_to_all(pieces, "aux", 1, 1, tiled=True)
    mine = pieces[:, :, : cols // n_aux].astype(jnp.float32).sum(1).astype(jnp.bfloat16)
    parts = pieces[:, :, cols // n_aux:].astype(jnp.float32)
    width = small.shape[1]
    small_sum = (parts[:, :, :width] + parts[:, :, width:]).sum(1)
    return lax.all_gather(mine, "aux", axis=1, tiled=True).astype(jnp.float32), small_sum


def _inverse_factor_kernel(gram_ref, inverse_ref):
    work = gram_ref[...]
    k = work.shape[0]
    rows = lax.broadcasted_iota(jnp.int32, (k, k), 0)
    lanes = lax.broadcasted_iota(jnp.int32, (k, k), 1)
    row_ids = lax.broadcasted_iota(jnp.int32, (k, 1), 0)
    lane_ids = lax.broadcasted_iota(jnp.int32, (1, k), 1)
    inverse = (rows == lanes).astype(jnp.float32)
    for j in range(k):
        pick = rows == j
        column = jnp.sum(jnp.where(lanes == j, work, 0.0), axis=1, keepdims=True)
        work_row = jnp.sum(jnp.where(pick, work, 0.0), axis=0, keepdims=True)
        inverse_row = jnp.sum(jnp.where(pick, inverse, 0.0), axis=0, keepdims=True)
        pivot = jnp.sum(jnp.where(lane_ids == j, work_row, 0.0), axis=1, keepdims=True)
        scale = 1.0 / jnp.sqrt(pivot)
        work_row = work_row * scale
        inverse_row = inverse_row * scale
        factor = jnp.where(row_ids > j, column * scale, 0.0)
        work = jnp.where(pick, work_row, work - factor * work_row)
        inverse = jnp.where(pick, inverse_row, inverse - factor * inverse_row)
    inverse_ref[...] = inverse

def inverse_factor(gram_now):
    k = gram_now.shape[0]
    return pl.pallas_call(
        _inverse_factor_kernel,
        out_shape=jax.ShapeDtypeStruct((k, k), jnp.float32),
        in_specs=[pl.BlockSpec(memory_space=pltpu.VMEM)],
        out_specs=pl.BlockSpec(memory_space=pltpu.VMEM),
    )(gram_now)


def on_device(b_tensor, eps_occ, eps_vir, trial):
    block_cols = b_tensor.shape[1]
    npair_all = eps_occ.shape[0] * eps_vir.shape[0]
    k = trial.shape[0]
    nvir = eps_vir.shape[0]
    if block_cols % nvir == 0:
        occ_rows = block_cols // nvir
        n_blocks = eps_occ.shape[0] // occ_rows
        mine = lax.broadcasted_iota(jnp.int32, (n_blocks, 1), 0) == lax.axis_index("pair")
        occ_block = jnp.sum(jnp.where(mine, eps_occ.reshape(n_blocks, occ_rows), 0.0), axis=0)
        diagonal = (eps_vir[None, :] - occ_block[:, None]).reshape(block_cols)
    else:
        everything = (eps_vir[None, :] - eps_occ[:, None]).reshape(npair_all)
        diagonal = lax.dynamic_slice_in_dim(
            everything, lax.axis_index("pair") * block_cols, block_cols)
    diag_row = diagonal[None, :]
    trial_now = trial
    for iteration in range(ITERS):
        wide_trial = trial_now.astype(jnp.float32)
        weighted = wide_trial * diag_row
        weighted_high, weighted_low = split_bf16(weighted)
        if iteration == 0:
            both = correlation_of(
                jnp.concatenate([trial_now, weighted_high, weighted_low], axis=0), trial_now, None)
            gram_part = both[:k]
            weighted_part = both[k:2 * k] + both[2 * k:]
            cross_part = correlation_of(b_tensor, trial_now, None)
        else:
            high, low = split_bf16(trial_now)
            split = jnp.concatenate([high, low], axis=0)
            both = correlation_of(
                jnp.concatenate([high, low, weighted_high, weighted_low], axis=0), split, None)
            gram_part = both[:k, :k] + both[:k, k:] + both[k:2 * k, :k]
            weighted_part = both[2 * k:3 * k, :k] + both[2 * k:3 * k, k:] + both[3 * k:, :k]
            cross = correlation_of(b_tensor, split, None)
            cross_part = cross[:, :k] + cross[:, k:]
        summed = pair_sum(jnp.concatenate(
            [gram_part / npair_all, weighted_part / npair_all, cross_part], axis=0))
        inverse = inverse_factor(summed[:k])
        basis_now = split_product(inverse, wide_trial)
        projected = lax.dot_general(
            summed[2 * k:], inverse, (((1,), (1,)), ((), ())),
            precision=HIGHEST_PRECISION, preferred_element_type=jnp.float32,
        )
        group_part = lax.dot_general(
            projected, projected, (((0,), (0,)), ((), ())),
            precision=HIGHEST_PRECISION, preferred_element_type=jnp.float32,
        )
        diag_part = product(product(inverse, summed[k:2 * k]), inverse.T)
        projected_low = projected.astype(jnp.bfloat16)
        term = lax.dot_general(
            projected_low, b_tensor, (((0,), (0,)), ((), ())), preferred_element_type=jnp.float32
        ).astype(jnp.bfloat16)
        coupling, group_sum = aux_sum(term, group_part / npair_all)
        subspace = group_sum + diag_part
        image_now = coupling + diag_row * basis_now
        residual = image_now - split_product(subspace, basis_now)
        trial_now = basis_now - residual / diag_row
    return (trial_now, residual.astype(jnp.bfloat16), subspace)


def solution(mesh):
    in_specs = (P("aux", "pair"), P(), P(), P(None, "pair"))
    out_specs = (P(None, "pair"), P(None, "pair"), P())
    return jax.shard_map(
        on_device, mesh=mesh, in_specs=in_specs, out_specs=out_specs, check_vma=False
    )
```

```python
import jax
import jax.numpy as jnp
from jax import lax
from jax.sharding import PartitionSpec as P
from jax.experimental import pallas as pl
from jax.experimental.pallas import tpu as pltpu

ITERS = 2


HIGHEST_PRECISION = lax.Precision.HIGHEST


def correlation_of(first_rows, second_rows, precision=HIGHEST_PRECISION):
    return lax.dot_general(
        first_rows,
        second_rows,
        (((1,), (1,)), ((), ())),
        precision=precision,
        preferred_element_type=jnp.float32,
    )


def product(first_mat, second_mat):
    return jnp.dot(
        first_mat, second_mat, precision=HIGHEST_PRECISION, preferred_element_type=jnp.float32
    )


def split_bf16(values):
    high_wide = lax.reduce_precision(values, exponent_bits=8, mantissa_bits=7)
    return high_wide.astype(jnp.bfloat16), (values - high_wide).astype(jnp.bfloat16)


def split_product(first_mat, second_mat):
    first_high, first_low = split_bf16(first_mat)
    second_high, second_low = split_bf16(second_mat)
    return jnp.dot(
        jnp.concatenate([first_high, first_low, first_high], axis=1),
        jnp.concatenate([second_high, second_high, second_low], axis=0),
        preferred_element_type=jnp.float32,
    )


def pair_sum(matrices):
    return lax.all_gather(matrices, "pair").sum(0)


def aux_sum(terms, small):
    n_aux = lax.axis_size("aux")
    rows, cols = terms.shape
    high, low = split_bf16(small)
    extra = jnp.concatenate([high, low], axis=1)
    pieces = jnp.concatenate([
        terms.reshape(rows, n_aux, cols // n_aux),
        jnp.broadcast_to(extra[:, None, :], (rows, n_aux, extra.shape[1])),
    ], axis=2)
    pieces = lax.all_to_all(pieces, "aux", 1, 1, tiled=True)
    mine = pieces[:, :, : cols // n_aux].astype(jnp.float32).sum(1).astype(jnp.bfloat16)
    parts = pieces[:, :, cols // n_aux:].astype(jnp.float32)
    width = small.shape[1]
    small_sum = (parts[:, :, :width] + parts[:, :, width:]).sum(1)
    return lax.all_gather(mine, "aux", axis=1, tiled=True).astype(jnp.float32), small_sum


def _inverse_factor_kernel(gram_ref, inverse_ref):
    work = gram_ref[...]
    k = work.shape[0]
    rows = lax.broadcasted_iota(jnp.int32, (k, k), 0)
    lanes = lax.broadcasted_iota(jnp.int32, (k, k), 1)
    row_ids = lax.broadcasted_iota(jnp.int32, (k, 1), 0)
    lane_ids = lax.broadcasted_iota(jnp.int32, (1, k), 1)
    inverse = (rows == lanes).astype(jnp.float32)
    for j in range(k):
        pick = rows == j
        column = jnp.sum(jnp.where(lanes == j, work, 0.0), axis=1, keepdims=True)
        work_row = jnp.sum(jnp.where(pick, work, 0.0), axis=0, keepdims=True)
        inverse_row = jnp.sum(jnp.where(pick, inverse, 0.0), axis=0, keepdims=True)
        pivot = jnp.sum(jnp.where(lane_ids == j, work_row, 0.0), axis=1, keepdims=True)
        scale = 1.0 / jnp.sqrt(pivot)
        work_row = work_row * scale
        inverse_row = inverse_row * scale
        factor = jnp.where(row_ids > j, column * scale, 0.0)
        work = jnp.where(pick, work_row, work - factor * work_row)
        inverse = jnp.where(pick, inverse_row, inverse - factor * inverse_row)
    inverse_ref[...] = inverse

def inverse_factor(gram_now):
    k = gram_now.shape[0]
    return pl.pallas_call(
        _inverse_factor_kernel,
        out_shape=jax.ShapeDtypeStruct((k, k), jnp.float32),
        in_specs=[pl.BlockSpec(memory_space=pltpu.VMEM)],
        out_specs=pl.BlockSpec(memory_space=pltpu.VMEM),
    )(gram_now)


def on_device(b_tensor, eps_occ, eps_vir, trial):
    block_cols = b_tensor.shape[1]
    npair_all = eps_occ.shape[0] * eps_vir.shape[0]
    k = trial.shape[0]
    nvir = eps_vir.shape[0]
    if block_cols % nvir == 0:
        occ_rows = block_cols // nvir
        occ_block = lax.dynamic_slice_in_dim(eps_occ, lax.axis_index("pair") * occ_rows, occ_rows)
        diagonal = (eps_vir[None, :] - occ_block[:, None]).reshape(block_cols)
    else:
        everything = (eps_vir[None, :] - eps_occ[:, None]).reshape(npair_all)
        diagonal = lax.dynamic_slice_in_dim(
            everything, lax.axis_index("pair") * block_cols, block_cols)
    diag_row = diagonal[None, :]
    trial_now = trial
    for iteration in range(ITERS):
        wide_trial = trial_now.astype(jnp.float32)
        weighted = wide_trial * diag_row
        weighted_high, weighted_low = split_bf16(weighted)
        if iteration == 0:
            rows = b_tensor.shape[0]
            summed = pair_sum(correlation_of(
                jnp.concatenate([b_tensor, trial_now, weighted_high, weighted_low], axis=0),
                trial_now, None))
            cross_sum = summed[:rows]
            gram_sum = summed[rows:rows + k] / npair_all
            weighted_sum = (summed[rows + k:rows + 2 * k] + summed[rows + 2 * k:]) / npair_all
        else:
            high, low = split_bf16(trial_now)
            split = jnp.concatenate([high, low], axis=0)
            both = correlation_of(
                jnp.concatenate([high, low, weighted_high, weighted_low], axis=0), split, None)
            gram_part = both[:k, :k] + both[:k, k:] + both[k:2 * k, :k]
            weighted_part = both[2 * k:3 * k, :k] + both[2 * k:3 * k, k:] + both[3 * k:, :k]
            cross = correlation_of(b_tensor, split, None)
            cross_part = cross[:, :k] + cross[:, k:]
            summed = pair_sum(jnp.concatenate(
                [gram_part / npair_all, weighted_part / npair_all, cross_part], axis=0))
            gram_sum = summed[:k]
            weighted_sum = summed[k:2 * k]
            cross_sum = summed[2 * k:]
        inverse = inverse_factor(gram_sum)
        basis_now = split_product(inverse, wide_trial)
        projected = lax.dot_general(
            cross_sum, inverse, (((1,), (1,)), ((), ())),
            precision=HIGHEST_PRECISION, preferred_element_type=jnp.float32,
        )
        group_part = lax.dot_general(
            projected, projected, (((0,), (0,)), ((), ())),
            precision=HIGHEST_PRECISION, preferred_element_type=jnp.float32,
        )
        diag_part = product(product(inverse, weighted_sum), inverse.T)
        projected_low = projected.astype(jnp.bfloat16)
        term = lax.dot_general(
            projected_low, b_tensor, (((0,), (0,)), ((), ())), preferred_element_type=jnp.float32
        ).astype(jnp.bfloat16)
        coupling, group_sum = aux_sum(term, group_part / npair_all)
        subspace = group_sum + diag_part
        image_now = coupling + diag_row * basis_now
        residual = image_now - split_product(subspace, basis_now)
        trial_now = basis_now - residual / diag_row
    return (trial_now, residual.astype(jnp.bfloat16), subspace)


def solution(mesh):
    in_specs = (P("aux", "pair"), P(), P(), P(None, "pair"))
    out_specs = (P(None, "pair"), P(None, "pair"), P())
    return jax.shard_map(
        on_device, mesh=mesh, in_specs=in_specs, out_specs=out_specs, check_vma=False
    )
```
